256 devices in a mesh: seq: 16 (over y, x), fsdp: 16 (over z, core).
Axes of the slice: x: 4, y: 4, z: 8, core: 2. Of those that a mesh axis runs over, the one named last changes fastest.
Arguments:
- byte_rows: bfloat16 [16, 16384, 512], P('fsdp', 'seq'), may hold values from -6 to 6
- cotangent: bfloat16 [16, 16384, 512], P('fsdp', 'seq'), may hold values from -6 to 6
- doc_ids: int32 [16, 16384], P('fsdp', 'seq'), may hold values from 0 to 31, never falling along the last dimension, each value on 1 to 2048 neighbouring positions
- conv_weight: bfloat16 [8, 32, 16, 16], replicated, may hold values from -0.5 to 0.5
- norm_gain: float32 [512], replicated, may hold values from 0.5 to 1.5
- proj_weight: bfloat16 [4096, 512], P('fsdp'), may hold values from -0.25 to 0.25
- round_seed: int32 [1], replicated, may hold values from 0 to 1073741823
- step_count: int32 [1], replicated, may hold values from 0 to 999999
Outputs:
- grad_bytes: float32 [16, 16384, 512], P('fsdp', 'seq')
- grad_proj: float32 [4096, 512], P('fsdp')
- grad_conv: float32 [8, 32, 16, 16], replicated
- grad_gain: float32 [512], replicated
The draws below stay inside these ranges and needn't reach their ends.
Inputs may be any that keep to these rules, and one draw needn't show every extreme that they name: `doc_ids`: along each sequence the document numbers never fall; no document covers more than 2048 bytes, and one covers exactly 2048.
All inputs are finite; a program needn't handle non-finite values.
Results may differ from the reference program's by a relative error of at most 0.0046.
Values may be sent and summed in bfloat16 or wider, within the bound.
No kernel may reach another device: no remote copies, remote signals or barrier semaphores. Data moves between devices by JAX's collectives and lax.ppermute only.
A program may use at most 128 MiB of HBM per device.

```python
import math
import jax
import jax.numpy as jnp
import numpy as np
from jax import lax

D = 512
GROUPS = 32
KERNEL = 8
STRIDE = 4
CG = 16
FF = 4096
LEN = 16384
SEQS = 16
DOCS = 32
DOC_MOST = 2048


def levels(stream_key, shape, shards, low, largest):
    gain = 1.0
    for axis_at, shards_of in shards:
        draws = jax.random.uniform(jax.random.fold_in(jax.random.fold_in(stream_key, 6), axis_at), (shards_of,), jnp.float32, low / len(shards), largest / len(shards))
        gain = gain * jnp.repeat(jnp.exp(draws), shape[axis_at] // shards_of).reshape((-1,) + (1,) * (len(shape) - 1 - axis_at))
    return gain


def length_profile(count, total, reach, skew):
    weights = [(1 << 20) // math.isqrt(rank ** skew) + 1 for rank in range(2, count + 1)]
    rest, counts = total - reach - (count - 1), [1] * (count - 1)
    while rest > 0:
        movable = [i for i in range(count - 1) if counts[i] < reach]
        mass, left = sum([weights[i] for i in movable]), rest
        for i in movable:
            extra = min(reach - counts[i], max(1, left * weights[i] // mass), rest)
            counts[i] = counts[i] + extra
            rest = rest - extra
    return np.array([reach] + counts)


def uneven_parts(stream_key, amount, total, bound, slope):
    if amount == 2:
        one = jax.random.randint(stream_key, (), max(1, total - bound), min(bound, total - 1) + 1)
        return jnp.stack([one, total - one])
    sizes = jnp.asarray(length_profile(amount, total, bound, slope), jnp.int32)
    couples = (amount - 1) // 2
    giver, receiver = sizes[1:1 + 2 * couples:2], sizes[2:2 + 2 * couples:2]
    slack = jnp.minimum(giver - 1, bound - receiver)
    passed = jax.random.randint(jax.random.fold_in(stream_key, 1), (couples,), 0, 1 << 20) % (slack + 1)
    sizes = sizes.at[1:1 + 2 * couples:2].set(giver - passed).at[2:2 + 2 * couples:2].set(receiver + passed)
    return sizes[jax.random.permutation(jax.random.fold_in(stream_key, 2), amount)]


def bell_draw(rng, shape, width, reach, pieces=(), kind=jnp.bfloat16):
    result = jax.random.normal(rng, shape, jnp.float32) * width
    if len(pieces) > 0:
        result = levels(rng, shape, pieces, -0.22, 0.18) * result
    return jnp.clip(result, min=-reach, max=reach).astype(kind)


def setup_inputs(seed: int = 0) -> dict:
    streams_of = jax.random.split(jax.random.key(seed), 9)
    return {
        "byte_rows": bell_draw(streams_of[0], (SEQS, LEN, D), 1.0, 6.0, ((0, 16), (1, 16))),
        "cotangent": bell_draw(streams_of[1], (SEQS, LEN, D), 1.0, 6.0, ((0, 16), (1, 16))),
        "doc_ids": jax.vmap(lambda own: jnp.searchsorted(jnp.cumsum(uneven_parts(own, DOCS, LEN, DOC_MOST, 2)), jnp.arange(LEN), side="right"))(jax.random.split(streams_of[2], SEQS)).reshape((SEQS, LEN)).astype(jnp.int32),
        "conv_weight": bell_draw(streams_of[3], (KERNEL, GROUPS, CG, CG), (KERNEL * CG) ** -0.5, 0.5),
        "norm_gain": jnp.clip(1.0 + 0.1 * jax.random.normal(streams_of[4], (D,), jnp.float32), 0.5, 1.5),
        "proj_weight": bell_draw(streams_of[5], (FF, D), D ** -0.5, 0.25, ((0, 16),)),
        "round_seed": jax.random.randint(streams_of[6], (1,), 0, 1073741824).astype(jnp.int32),
        "step_count": jax.random.randint(streams_of[7], (1,), 0, 1000000).astype(jnp.int32),
    }


GELU_A = 0.7978845608028654
GELU_B = 0.044715
QUANT = 0.25

def gelu_grad(values):
    tangent = jnp.tanh(GELU_A * (values + GELU_B * values * values * values))
    return 0.5 * (1.0 + tangent) + 0.5 * values * (1.0 - tangent * tangent) * GELU_A * (1.0 + 3.0 * GELU_B * values * values)

def mix_bits(flat_index, seed_value, step_value):
    hashed = flat_index * jnp.int32(-1640531535) + seed_value * jnp.int32(-2048144777) + step_value * jnp.int32(-1028477379)
    hashed = hashed ^ lax.shift_right_logical(hashed, jnp.int32(16))
    hashed = hashed * jnp.int32(2146121005)
    hashed = hashed ^ lax.shift_right_logical(hashed, jnp.int32(15))
    hashed = hashed * jnp.int32(-2073254261)
    hashed = hashed ^ lax.shift_right_logical(hashed, jnp.int32(16))
    return lax.shift_right_logical(hashed, jnp.int32(8)).astype(jnp.float32) / 16777216.0

def tap_windows(series, extra_rows, patches):
    joined = jnp.concatenate([series, extra_rows], 0)
    tail_shape = joined.shape[1:]
    lower = joined[:-STRIDE].reshape((patches, STRIDE) + tail_shape)
    upper = joined[STRIDE:].reshape((patches, STRIDE) + tail_shape)
    return jnp.concatenate([lower, upper], 1)

def one_sequence(byte_block, upstream, doc_block, conv_weight, norm_gain, proj_weight):
    length = byte_block.shape[0]
    patches = length // STRIDE
    pad_rows = jnp.zeros((STRIDE, D), jnp.bfloat16)
    pad_docs = jnp.zeros((STRIDE,), jnp.int32)
    window = tap_windows(byte_block, pad_rows, patches)
    up_window = tap_windows(upstream, pad_rows, patches)
    doc_window = tap_windows(doc_block, pad_docs, patches)
    position = STRIDE * jnp.arange(patches, dtype=jnp.int32)[:, None] + jnp.arange(KERNEL, dtype=jnp.int32)[None, :]
    keep_tap = (doc_window == doc_window[:, :1]) & (position < length)
    keep_f = keep_tap.astype(jnp.float32)[:, :, None]
    masked = (window.astype(jnp.float32) * keep_f).astype(jnp.bfloat16)
    grouped = masked.reshape(patches, KERNEL, GROUPS, CG).astype(jnp.float32)
    conv_f = conv_weight.astype(jnp.float32)
    hidden = jnp.einsum('pkgc,kgcd->pgd', grouped, conv_f).reshape(patches, D)
    factor = lax.rsqrt(lax.optimization_barrier(jnp.mean(hidden * hidden, axis=-1, keepdims=True)) + 1e-06)
    normed = (hidden * factor * norm_gain).astype(jnp.bfloat16)
    pre_act = jnp.dot(normed, proj_weight.T, preferred_element_type=jnp.float32)
    grad_pre = up_window.astype(jnp.float32) * keep_f * gelu_grad(pre_act.reshape(patches, KERNEL, D))
    grad_pre = grad_pre.reshape(patches, FF).astype(jnp.bfloat16)
    grad_norm = jnp.dot(grad_pre, proj_weight, preferred_element_type=jnp.float32)
    proj_part = jnp.dot(grad_pre.T, normed, preferred_element_type=jnp.float32)
    gain_part = lax.optimization_barrier(jnp.sum(grad_norm * hidden * factor, axis=0))
    gained = norm_gain * grad_norm
    grad_hidden = factor * gained - hidden * factor * factor * factor * lax.optimization_barrier(jnp.mean(gained * hidden, axis=-1, keepdims=True))
    grad_hidden = grad_hidden.reshape(patches, GROUPS, CG)
    conv_part = jnp.einsum('pkgc,pgd->kgcd', grouped, grad_hidden, precision=lax.Precision.HIGHEST)
    grad_window = jnp.einsum('pgd,kgcd->pkgc', grad_hidden, conv_f, precision=lax.Precision.HIGHEST)
    grad_window = grad_window.reshape(patches, KERNEL, D) * keep_f
    back_rows = jnp.zeros((length + STRIDE, D), jnp.float32)
    back_rows = back_rows.at[:length].add(grad_window[:, :STRIDE].reshape(length, D))
    back_rows = back_rows.at[STRIDE:].add(grad_window[:, STRIDE:].reshape(length, D))
    grad_rows = upstream.astype(jnp.float32) + back_rows[:length]
    return (grad_rows, proj_part, gain_part, conv_part)

def reference(byte_rows, cotangent, doc_ids, conv_weight, norm_gain, proj_weight, round_seed, step_count):

    def visit(carry, inputs):
        grad_rows, proj_part, gain_part, conv_part = one_sequence(inputs[0], inputs[1], inputs[2], conv_weight, norm_gain, proj_weight)
        return ((carry[0] + proj_part, carry[1] + gain_part, carry[2] + conv_part), grad_rows)
    start_carry = (jnp.zeros((FF, D), jnp.float32), jnp.zeros((D,), jnp.float32), jnp.zeros((KERNEL, GROUPS, CG, CG), jnp.float32))
    sums, grad_bytes = lax.scan(visit, start_carry, (byte_rows, cotangent, doc_ids))
    grad_scale = 1.0 / math.sqrt(SEQS * LEN // STRIDE)
    flat_index = jnp.arange(FF, dtype=jnp.int32)[:, None] * jnp.int32(D) + jnp.arange(D, dtype=jnp.int32)[None, :]
    dither_noise = mix_bits(flat_index, round_seed[0], step_count[0])
    grad_proj = sums[0] * grad_scale + QUANT * (dither_noise - 0.5)
    return (grad_bytes, grad_proj, sums[2] * grad_scale, sums[1] * grad_scale)
```

```python
import math

import jax
import jax.numpy as jnp
from jax import lax
from jax.sharding import PartitionSpec as P

GROUPS = 32
KERNEL = 8
STRIDE = 4
CG = 16


GELU_A = 0.7978845608028654
GELU_B = 0.044715
QUANT = 0.25


def shifted(value, axis, steps):
    count = lax.axis_size(axis)
    initial, last = (max(0, -steps), min(count, count - steps))
    return lax.ppermute(value, axis, [(source, source + steps) for source in range(initial, last)])


def gelu_grad(values):
    tangent = jnp.tanh(GELU_A * (values + GELU_B * values * values * values))
    return 0.5 * (1.0 + tangent) + 0.5 * values * (1.0 - tangent * tangent) * GELU_A * (
        1.0 + 3.0 * GELU_B * values * values
    )


def mix_bits(flat_index, seed_value, step_value):
    hashed = (
        flat_index * jnp.int32(-1640531535)
        + seed_value * jnp.int32(-2048144777)
        + step_value * jnp.int32(-1028477379)
    )
    hashed = hashed ^ lax.shift_right_logical(hashed, jnp.int32(16))
    hashed = hashed * jnp.int32(2146121005)
    hashed = hashed ^ lax.shift_right_logical(hashed, jnp.int32(15))
    hashed = hashed * jnp.int32(-2073254261)
    hashed = hashed ^ lax.shift_right_logical(hashed, jnp.int32(16))
    return lax.shift_right_logical(hashed, jnp.int32(8)).astype(jnp.float32) / 16777216.0


def split_bf16(value):
    high = value.astype(jnp.bfloat16)
    low = (value - high.astype(jnp.float32)).astype(jnp.bfloat16)
    return high, low


def dot_f32(lhs, rhs, dims):
    return lax.dot_general(lhs, rhs, (dims, ((), ())), preferred_element_type=jnp.float32)


def per_device(
    byte_rows, cotangent, doc_ids, conv_weight, norm_gain, proj_weight, round_seed, step_count
):
    byte_block = byte_rows[0]
    upstream = cotangent[0]
    doc_block = doc_ids[0]
    length = byte_block.shape[0]
    row_width = byte_block.shape[1]
    patches = length // STRIDE
    half = STRIDE * row_width
    panel_rows = proj_weight.shape[0]
    next_bytes, next_up, next_docs = shifted(
        (byte_block[:STRIDE], upstream[:STRIDE], doc_block[:STRIDE]), "seq", -1
    )
    bytes_lo = byte_block.reshape(patches, half)
    bytes_hi = jnp.concatenate([bytes_lo[1:], next_bytes.reshape(1, half)], 0)
    up_lo = upstream.reshape(patches, half)
    up_hi = jnp.concatenate([up_lo[1:], next_up.reshape(1, half)], 0)
    docs_lo = doc_block.reshape(patches, STRIDE)
    docs_hi = jnp.concatenate([docs_lo[1:], next_docs.reshape(1, STRIDE)], 0)
    is_last = lax.axis_index("seq") == lax.axis_size("seq") - 1
    patch_ids = lax.broadcasted_iota(jnp.int32, (patches, STRIDE), 0)
    spilled = is_last & (patch_ids == patches - 1)
    keep_lo = docs_lo == docs_lo[:, :1]
    keep_hi = (docs_hi == docs_lo[:, :1]) & jnp.logical_not(spilled)

    def spread(keep):
        return jnp.broadcast_to(keep[:, :, None], (patches, STRIDE, row_width)).reshape(
            patches, half
        )

    keep_lo_f = spread(keep_lo.astype(jnp.float32))
    keep_hi_f = spread(keep_hi.astype(jnp.float32))
    win_lo = bytes_lo * keep_lo_f.astype(jnp.bfloat16)
    win_hi = bytes_hi * keep_hi_f.astype(jnp.bfloat16)

    group_eye = jnp.eye(GROUPS, dtype=jnp.bfloat16)
    dense_weight = (
        conv_weight[:, :, :, None, :] * group_eye[None, :, None, :, None]
    ).reshape(KERNEL, row_width, row_width)
    weight_lo = dense_weight[:STRIDE].reshape(half, row_width)
    weight_hi = dense_weight[STRIDE:].reshape(half, row_width)

    hidden = dot_f32(win_lo, weight_lo, ((1,), (0,))) + dot_f32(win_hi, weight_hi, ((1,), (0,)))
    factor = lax.rsqrt(jnp.mean(hidden * hidden, axis=-1, keepdims=True) + 1e-06)
    normed = (hidden * factor * norm_gain).astype(jnp.bfloat16)

    full_proj = lax.all_gather(proj_weight, "fsdp", axis=0, tiled=True)
    proj_lo = full_proj[:half]
    proj_hi = full_proj[half:]
    pre_lo = dot_f32(normed, proj_lo, ((1,), (1,)))
    pre_hi = dot_f32(normed, proj_hi, ((1,), (1,)))
    grad_pre_lo = (up_lo.astype(jnp.float32) * keep_lo_f * gelu_grad(pre_lo)).astype(jnp.bfloat16)
    grad_pre_hi = (up_hi.astype(jnp.float32) * keep_hi_f * gelu_grad(pre_hi)).astype(jnp.bfloat16)

    proj_part = jnp.concatenate(
        [dot_f32(grad_pre_lo, normed, ((0,), (0,))), dot_f32(grad_pre_hi, normed, ((0,), (0,)))], 0
    )
    panel_part = lax.psum_scatter(proj_part, "fsdp", scatter_dimension=0, tiled=True)

    grad_norm = dot_f32(grad_pre_lo, proj_lo, ((1,), (0,))) + dot_f32(
        grad_pre_hi, proj_hi, ((1,), (0,))
    )
    gain_part = jnp.sum(grad_norm * hidden * factor, axis=0)
    gained = norm_gain * grad_norm
    grad_hidden = factor * gained - hidden * factor * factor * factor * jnp.mean(
        gained * hidden, axis=-1, keepdims=True
    )
    gh_high, gh_low = split_bf16(grad_hidden)

    def window_grad(window):
        full = dot_f32(window, gh_high, ((0,), (0,))) + dot_f32(window, gh_low, ((0,), (0,)))
        blocks = full.reshape(STRIDE, GROUPS, CG, GROUPS, CG)
        mask = jnp.eye(GROUPS, dtype=jnp.float32)[None, :, None, :, None]
        return jnp.sum(blocks * mask, axis=3)

    conv_part = jnp.concatenate([window_grad(win_lo), window_grad(win_hi)], 0)

    def back_taps(weight, keep_f):
        taps = dot_f32(gh_high, weight, ((1,), (1,))) + dot_f32(gh_low, weight, ((1,), (1,)))
        return (taps * keep_f).reshape(length, row_width)

    back_lower = back_taps(weight_lo, keep_lo_f)
    back_upper = back_taps(weight_hi, keep_hi_f)
    incoming = shifted(back_upper[length - STRIDE :], "seq", 1)
    back_rows = back_lower + jnp.concatenate([incoming, back_upper[: length - STRIDE]], 0)
    grad_bytes = (upstream.astype(jnp.float32) + back_rows)[None]

    conv_size = conv_part.size
    small = jnp.concatenate([conv_part.reshape(-1), gain_part]).reshape(-1, row_width)
    small = lax.psum(small, "fsdp")
    joined = lax.psum(jnp.concatenate([panel_part, small], 0), "seq")
    proj_sum = joined[:panel_rows]
    small_sum = joined[panel_rows:].reshape(-1)
    conv_sum = small_sum[:conv_size].reshape(conv_part.shape)
    gain_sum = small_sum[conv_size:]

    total_patches = patches * lax.axis_size("seq") * lax.axis_size("fsdp")
    grad_scale = 1.0 / math.sqrt(total_patches)
    first_panel = lax.axis_index("fsdp") * jnp.int32(panel_rows)
    row_index = first_panel + jnp.arange(panel_rows, dtype=jnp.int32)
    flat_index = (
        row_index[:, None] * jnp.int32(row_width) + jnp.arange(row_width, dtype=jnp.int32)[None, :]
    )
    dither_noise = mix_bits(flat_index, round_seed[0], step_count[0])
    grad_proj = proj_sum * grad_scale + QUANT * (dither_noise - 0.5)
    return (grad_bytes, grad_proj, conv_sum * grad_scale, gain_sum * grad_scale)


def solution(mesh):
    in_specs = (
        P("fsdp", "seq", None),
        P("fsdp", "seq", None),
        P("fsdp", "seq"),
        P(),
        P(),
        P("fsdp", None),
        P(),
        P(),
    )
    out_specs = (P("fsdp", "seq", None), P("fsdp", None), P(), P())
    return jax.shard_map(
        per_device, mesh=mesh, in_specs=in_specs, out_specs=out_specs, check_vma=False
    )
```

```python
import math

import jax
import jax.numpy as jnp
from jax import lax
from jax.sharding import PartitionSpec as P

GROUPS = 32
KERNEL = 8
STRIDE = 4
CG = 16


GELU_A = 0.7978845608028654
GELU_B = 0.044715
QUANT = 0.25


def shifted(value, axis, steps):
    count = lax.axis_size(axis)
    initial, last = (max(0, -steps), min(count, count - steps))
    return lax.ppermute(value, axis, [(source, source + steps) for source in range(initial, last)])


def gelu_grad(values):
    tangent = jnp.tanh(GELU_A * (values + GELU_B * values * values * values))
    return 0.5 * (1.0 + tangent) + 0.5 * values * (1.0 - tangent * tangent) * GELU_A * (
        1.0 + 3.0 * GELU_B * values * values
    )


def mix_bits(flat_index, seed_value, step_value):
    hashed = (
        flat_index * jnp.int32(-1640531535)
        + seed_value * jnp.int32(-2048144777)
        + step_value * jnp.int32(-1028477379)
    )
    hashed = hashed ^ lax.shift_right_logical(hashed, jnp.int32(16))
    hashed = hashed * jnp.int32(2146121005)
    hashed = hashed ^ lax.shift_right_logical(hashed, jnp.int32(15))
    hashed = hashed * jnp.int32(-2073254261)
    hashed = hashed ^ lax.shift_right_logical(hashed, jnp.int32(16))
    return lax.shift_right_logical(hashed, jnp.int32(8)).astype(jnp.float32) / 16777216.0


def butterfly_sum(value, axis):
    count = lax.axis_size(axis)
    distance = 1
    while distance < count:
        partner = lax.ppermute(value, axis, [(i, i ^ distance) for i in range(count)])
        value = value + partner
        distance *= 2
    return value


def split_bf16(value):
    high = lax.reduce_precision(value, exponent_bits=8, mantissa_bits=7)
    low = (value - high).astype(jnp.bfloat16)
    return high.astype(jnp.bfloat16), low


def dot_f32(lhs, rhs, dims):
    return lax.dot_general(lhs, rhs, (dims, ((), ())), preferred_element_type=jnp.float32)


def per_device(
    byte_rows, cotangent, doc_ids, conv_weight, norm_gain, proj_weight, round_seed, step_count
):
    byte_block = byte_rows[0]
    upstream = cotangent[0]
    doc_block = doc_ids[0]
    length = byte_block.shape[0]
    row_width = byte_block.shape[1]
    patches = length // STRIDE
    half = STRIDE * row_width
    panel_rows = proj_weight.shape[0]
    next_bytes, next_up, next_docs = shifted(
        (byte_block[:STRIDE], upstream[:STRIDE], doc_block[:STRIDE]), "seq", -1
    )
    bytes_lo = byte_block.reshape(patches, half)
    bytes_hi = jnp.concatenate([bytes_lo[1:], next_bytes.reshape(1, half)], 0)
    up_lo = upstream.reshape(patches, half)
    up_hi = jnp.concatenate([up_lo[1:], next_up.reshape(1, half)], 0)
    docs_lo = doc_block.reshape(patches, STRIDE)
    docs_hi = jnp.concatenate([docs_lo[1:], next_docs.reshape(1, STRIDE)], 0)
    is_last = lax.axis_index("seq") == lax.axis_size("seq") - 1
    patch_ids = lax.broadcasted_iota(jnp.int32, (patches, STRIDE), 0)
    spilled = is_last & (patch_ids == patches - 1)
    keep_lo = docs_lo == docs_lo[:, :1]
    keep_hi = (docs_hi == docs_lo[:, :1]) & jnp.logical_not(spilled)

    def spread(keep):
        return jnp.broadcast_to(keep[:, :, None], (patches, STRIDE, row_width)).reshape(
            patches, half
        )

    keep_lo_f = spread(keep_lo.astype(jnp.float32))
    keep_hi_f = spread(keep_hi.astype(jnp.float32))
    win_lo = bytes_lo * keep_lo_f.astype(jnp.bfloat16)
    win_hi = bytes_hi * keep_hi_f.astype(jnp.bfloat16)

    tile_rows = lax.broadcasted_iota(jnp.int32, (CG, row_width), 0)
    tile_cols = lax.broadcasted_iota(jnp.int32, (CG, row_width), 1)
    tiler = (tile_cols % CG == tile_rows).astype(jnp.bfloat16)
    tiled = dot_f32(conv_weight.reshape(KERNEL * row_width, CG), tiler, ((1,), (0,)))
    block_rows = lax.broadcasted_iota(jnp.int32, (half, row_width), 0)
    block_cols = lax.broadcasted_iota(jnp.int32, (half, row_width), 1)
    on_block = (block_rows % row_width) // CG == block_cols // CG
    dense_weight = tiled.reshape(2, half, row_width)
    weight_lo = jnp.where(on_block, dense_weight[0], 0.0).astype(jnp.bfloat16)
    weight_hi = jnp.where(on_block, dense_weight[1], 0.0).astype(jnp.bfloat16)

    hidden = dot_f32(win_lo, weight_lo, ((1,), (0,))) + dot_f32(win_hi, weight_hi, ((1,), (0,)))
    factor = lax.rsqrt(jnp.mean(hidden * hidden, axis=-1, keepdims=True) + 1e-06)
    normed = (hidden * factor * norm_gain).astype(jnp.bfloat16)

    full_proj = lax.all_gather(proj_weight, "fsdp", axis=0, tiled=True)
    proj_lo = full_proj[:half]
    proj_hi = full_proj[half:]
    pre_lo = dot_f32(normed, proj_lo, ((1,), (1,)))
    pre_hi = dot_f32(normed, proj_hi, ((1,), (1,)))
    grad_pre_lo = (up_lo.astype(jnp.float32) * keep_lo_f * gelu_grad(pre_lo)).astype(jnp.bfloat16)
    grad_pre_hi = (up_hi.astype(jnp.float32) * keep_hi_f * gelu_grad(pre_hi)).astype(jnp.bfloat16)

    proj_part = jnp.concatenate(
        [dot_f32(grad_pre_lo, normed, ((0,), (0,))), dot_f32(grad_pre_hi, normed, ((0,), (0,)))], 0
    )
    panel_part = lax.psum_scatter(proj_part, "fsdp", scatter_dimension=0, tiled=True)

    grad_norm = dot_f32(grad_pre_lo, proj_lo, ((1,), (0,))) + dot_f32(
        grad_pre_hi, proj_hi, ((1,), (0,))
    )
    gain_part = jnp.sum(grad_norm * hidden * factor, axis=0)
    gained = norm_gain * grad_norm
    grad_hidden = factor * gained - hidden * factor * factor * factor * jnp.mean(
        gained * hidden, axis=-1, keepdims=True
    )
    gh_high, gh_low = split_bf16(grad_hidden)

    def window_grad(window):
        full = dot_f32(window, gh_high, ((0,), (0,))) + dot_f32(window, gh_low, ((0,), (0,)))
        diagonal = lax.dot_general(
            jnp.where(on_block, full, 0.0),
            tiler.astype(jnp.float32),
            (((1,), (1,)), ((), ())),
            precision=lax.Precision.HIGHEST,
            preferred_element_type=jnp.float32,
        )
        return diagonal.reshape(STRIDE, GROUPS, CG, CG)

    conv_part = jnp.concatenate([window_grad(win_lo), window_grad(win_hi)], 0)

    def back_taps(weight, keep_f):
        taps = dot_f32(gh_high, weight, ((1,), (1,))) + dot_f32(gh_low, weight, ((1,), (1,)))
        return (taps * keep_f).reshape(length, row_width)

    back_lower = back_taps(weight_lo, keep_lo_f)
    back_upper = back_taps(weight_hi, keep_hi_f)
    incoming = shifted(back_upper[length - STRIDE :], "seq", 1)
    back_rows = back_lower + jnp.concatenate([incoming, back_upper[: length - STRIDE]], 0)
    grad_bytes = (upstream.astype(jnp.float32) + back_rows)[None]

    conv_size = conv_part.size
    small = jnp.concatenate([conv_part.reshape(-1), gain_part]).reshape(-1, row_width)
    small_sum = butterfly_sum(butterfly_sum(small, "fsdp"), "seq").reshape(-1)
    proj_sum = butterfly_sum(panel_part, "seq")
    conv_sum = small_sum[:conv_size].reshape(conv_part.shape)
    gain_sum = small_sum[conv_size:]

    total_patches = patches * lax.axis_size("seq") * lax.axis_size("fsdp")
    grad_scale = 1.0 / math.sqrt(total_patches)
    first_panel = lax.axis_index("fsdp") * jnp.int32(panel_rows)
    row_index = first_panel + jnp.arange(panel_rows, dtype=jnp.int32)
    flat_index = (
        row_index[:, None] * jnp.int32(row_width) + jnp.arange(row_width, dtype=jnp.int32)[None, :]
    )
    dither_noise = mix_bits(flat_index, round_seed[0], step_count[0])
    grad_proj = proj_sum * grad_scale + QUANT * (dither_noise - 0.5)
    return (grad_bytes, grad_proj, conv_sum * grad_scale, gain_sum * grad_scale)


def solution(mesh):
    in_specs = (
        P("fsdp", "seq", None),
        P("fsdp", "seq", None),
        P("fsdp", "seq"),
        P(),
        P(),
        P("fsdp", None),
        P(),
        P(),
    )
    out_specs = (P("fsdp", "seq", None), P("fsdp", None), P(), P())
    return jax.shard_map(
        per_device, mesh=mesh, in_specs=in_specs, out_specs=out_specs, check_vma=False
    )
```

```python
import math

import jax
import jax.numpy as jnp
from jax import lax
from jax.sharding import PartitionSpec as P

GROUPS = 32
KERNEL = 8
STRIDE = 4
CG = 16


GELU_A = 0.7978845608028654
GELU_B = 0.044715
QUANT = 0.25


def shifted(value, axis, steps):
    count = lax.axis_size(axis)
    initial, last = (max(0, -steps), min(count, count - steps))
    return lax.ppermute(value, axis, [(source, source + steps) for source in range(initial, last)])


def gelu_grad(values):
    tangent = jnp.tanh(GELU_A * (values + GELU_B * values * values * values))
    return 0.5 * (1.0 + tangent) + 0.5 * values * (1.0 - tangent * tangent) * GELU_A * (
        1.0 + 3.0 * GELU_B * values * values
    )


def mix_bits(flat_index, seed_value, step_value):
    hashed = (
        flat_index * jnp.int32(-1640531535)
        + seed_value * jnp.int32(-2048144777)
        + step_value * jnp.int32(-1028477379)
    )
    hashed = hashed ^ lax.shift_right_logical(hashed, jnp.int32(16))
    hashed = hashed * jnp.int32(2146121005)
    hashed = hashed ^ lax.shift_right_logical(hashed, jnp.int32(15))
    hashed = hashed * jnp.int32(-2073254261)
    hashed = hashed ^ lax.shift_right_logical(hashed, jnp.int32(16))
    return lax.shift_right_logical(hashed, jnp.int32(8)).astype(jnp.float32) / 16777216.0


def butterfly_sum(value, axis, first=0, last=None):
    count = lax.axis_size(axis)
    last = count.bit_length() - 1 if last is None else last
    for level in range(first, last):
        distance = 1 << level
        partner = lax.ppermute(value, axis, [(i, i ^ distance) for i in range(count)])
        value = value + partner
    return value


def split_bf16(value):
    high = lax.reduce_precision(value, exponent_bits=8, mantissa_bits=7)
    low = (value - high).astype(jnp.bfloat16)
    return high.astype(jnp.bfloat16), low


def dot_f32(lhs, rhs, dims):
    return lax.dot_general(lhs, rhs, (dims, ((), ())), preferred_element_type=jnp.float32)


def per_device(
    byte_rows, cotangent, doc_ids, conv_weight, norm_gain, proj_weight, round_seed, step_count
):
    byte_block = byte_rows[0]
    upstream = cotangent[0]
    doc_block = doc_ids[0]
    length = byte_block.shape[0]
    row_width = byte_block.shape[1]
    patches = length // STRIDE
    half = STRIDE * row_width
    panel_rows = proj_weight.shape[0]
    next_bytes, next_up, next_docs = shifted(
        (byte_block[:STRIDE], upstream[:STRIDE], doc_block[:STRIDE]), "seq", -1
    )
    bytes_lo = byte_block.reshape(patches, half)
    bytes_hi = jnp.concatenate([bytes_lo[1:], next_bytes.reshape(1, half)], 0)
    up_lo = upstream.reshape(patches, half)
    up_hi = jnp.concatenate([up_lo[1:], next_up.reshape(1, half)], 0)
    docs_lo = doc_block.reshape(patches, STRIDE)
    docs_hi = jnp.concatenate([docs_lo[1:], next_docs.reshape(1, STRIDE)], 0)
    is_last = lax.axis_index("seq") == lax.axis_size("seq") - 1
    patch_ids = lax.broadcasted_iota(jnp.int32, (patches, STRIDE), 0)
    spilled = is_last & (patch_ids == patches - 1)
    keep_lo = docs_lo == docs_lo[:, :1]
    keep_hi = (docs_hi == docs_lo[:, :1]) & jnp.logical_not(spilled)

    def spread(keep):
        return jnp.broadcast_to(keep[:, :, None], (patches, STRIDE, row_width)).reshape(
            patches, half
        )

    keep_lo_f = spread(keep_lo.astype(jnp.float32))
    keep_hi_f = spread(keep_hi.astype(jnp.float32))
    win_lo = bytes_lo * keep_lo_f.astype(jnp.bfloat16)
    win_hi = bytes_hi * keep_hi_f.astype(jnp.bfloat16)

    tile_rows = lax.broadcasted_iota(jnp.int32, (CG, row_width), 0)
    tile_cols = lax.broadcasted_iota(jnp.int32, (CG, row_width), 1)
    tiler = (tile_cols % CG == tile_rows).astype(jnp.bfloat16)
    tiled = dot_f32(conv_weight.reshape(KERNEL * row_width, CG), tiler, ((1,), (0,)))
    block_rows = lax.broadcasted_iota(jnp.int32, (half, row_width), 0)
    block_cols = lax.broadcasted_iota(jnp.int32, (half, row_width), 1)
    on_block = (block_rows % row_width) // CG == block_cols // CG
    dense_weight = tiled.reshape(2, half, row_width)
    weight_lo = jnp.where(on_block, dense_weight[0], 0.0).astype(jnp.bfloat16)
    weight_hi = jnp.where(on_block, dense_weight[1], 0.0).astype(jnp.bfloat16)

    hidden = dot_f32(win_lo, weight_lo, ((1,), (0,))) + dot_f32(win_hi, weight_hi, ((1,), (0,)))
    factor = lax.rsqrt(jnp.mean(hidden * hidden, axis=-1, keepdims=True) + 1e-06)
    normed = (hidden * factor * norm_gain).astype(jnp.bfloat16)

    full_proj = lax.all_gather(proj_weight, "fsdp", axis=0, tiled=True)
    pre_act = dot_f32(normed, full_proj, ((1,), (1,)))
    up_window = jnp.concatenate([up_lo, up_hi], 1).astype(jnp.float32)
    keep_f = jnp.concatenate([keep_lo_f, keep_hi_f], 1)
    grad_pre = (up_window * keep_f * gelu_grad(pre_act)).astype(jnp.bfloat16)

    column_half = row_width // 2
    panel_parts = [
        lax.psum_scatter(
            dot_f32(grad_pre, normed[:, part * column_half : (part + 1) * column_half], ((0,), (0,))),
            "fsdp",
            scatter_dimension=0,
            tiled=True,
        )
        for part in range(2)
    ]

    grad_norm = dot_f32(grad_pre, full_proj, ((1,), (0,)))
    gain_part = jnp.sum(grad_norm * hidden * factor, axis=0)
    gained = norm_gain * grad_norm
    grad_hidden = factor * gained - hidden * factor * factor * factor * jnp.mean(
        gained * hidden, axis=-1, keepdims=True
    )
    gh_high, gh_low = split_bf16(grad_hidden)

    def window_grad(window):
        full = dot_f32(window, gh_high, ((0,), (0,))) + dot_f32(window, gh_low, ((0,), (0,)))
        diagonal = lax.dot_general(
            jnp.where(on_block, full, 0.0),
            tiler.astype(jnp.float32),
            (((1,), (1,)), ((), ())),
            precision=lax.Precision.HIGHEST,
            preferred_element_type=jnp.float32,
        )
        return diagonal.reshape(STRIDE, GROUPS, CG, CG)

    conv_part = jnp.concatenate([window_grad(win_lo), window_grad(win_hi)], 0)

    def back_taps(weight, keep_f):
        taps = dot_f32(gh_high, weight, ((1,), (1,))) + dot_f32(gh_low, weight, ((1,), (1,)))
        return (taps * keep_f).reshape(length, row_width)

    back_lower = back_taps(weight_lo, keep_lo_f)
    back_upper = back_taps(weight_hi, keep_hi_f)
    incoming = shifted(back_upper[length - STRIDE :], "seq", 1)
    back_rows = back_lower + jnp.concatenate([incoming, back_upper[: length - STRIDE]], 0)
    grad_bytes = (upstream.astype(jnp.float32) + back_rows)[None]

    conv_size = conv_part.size
    small = jnp.concatenate([conv_part.reshape(-1), gain_part]).reshape(-1, row_width)
    small_sum = butterfly_sum(butterfly_sum(small, "fsdp"), "seq").reshape(-1)
    first_half = butterfly_sum(panel_parts[0], "seq", 0, 2)
    first_half, second_half = lax.optimization_barrier((first_half, panel_parts[1]))
    first_half = butterfly_sum(first_half, "seq", 2)
    second_half = butterfly_sum(second_half, "seq")
    proj_sum = jnp.concatenate([first_half, second_half], 1)
    conv_sum = small_sum[:conv_size].reshape(conv_part.shape)
    gain_sum = small_sum[conv_size:]

    total_patches = patches * lax.axis_size("seq") * lax.axis_size("fsdp")
    grad_scale = 1.0 / math.sqrt(total_patches)
    first_panel = lax.axis_index("fsdp") * jnp.int32(panel_rows)
    row_index = first_panel + jnp.arange(panel_rows, dtype=jnp.int32)
    flat_index = (
        row_index[:, None] * jnp.int32(row_width) + jnp.arange(row_width, dtype=jnp.int32)[None, :]
    )
    dither_noise = mix_bits(flat_index, round_seed[0], step_count[0])
    grad_proj = proj_sum * grad_scale + QUANT * (dither_noise - 0.5)
    return (grad_bytes, grad_proj, conv_sum * grad_scale, gain_sum * grad_scale)


def solution(mesh):
    in_specs = (
        P("fsdp", "seq", None),
        P("fsdp", "seq", None),
        P("fsdp", "seq"),
        P(),
        P(),
        P("fsdp", None),
        P(),
        P(),
    )
    out_specs = (P("fsdp", "seq", None), P("fsdp", None), P(), P())
    return jax.shard_map(
        per_device, mesh=mesh, in_specs=in_specs, out_specs=out_specs, check_vma=False
    )
```

```python
import math

import jax
import jax.numpy as jnp
from jax import lax
from jax.sharding import PartitionSpec as P

GROUPS = 32
KERNEL = 8
STRIDE = 4
CG = 16


GELU_A = 0.7978845608028654
GELU_B = 0.044715
QUANT = 0.25


def shifted(value, axis, steps):
    count = lax.axis_size(axis)
    initial, last = (max(0, -steps), min(count, count - steps))
    return lax.ppermute(value, axis, [(source, source + steps) for source in range(initial, last)])


def gelu_grad(values):
    tangent = jnp.tanh(GELU_A * (values + GELU_B * values * values * values))
    return 0.5 * (1.0 + tangent) + 0.5 * values * (1.0 - tangent * tangent) * GELU_A * (
        1.0 + 3.0 * GELU_B * values * values
    )


def mix_bits(flat_index, seed_value, step_value):
    hashed = (
        flat_index * jnp.int32(-1640531535)
        + seed_value * jnp.int32(-2048144777)
        + step_value * jnp.int32(-1028477379)
    )
    hashed = hashed ^ lax.shift_right_logical(hashed, jnp.int32(16))
    hashed = hashed * jnp.int32(2146121005)
    hashed = hashed ^ lax.shift_right_logical(hashed, jnp.int32(15))
    hashed = hashed * jnp.int32(-2073254261)
    hashed = hashed ^ lax.shift_right_logical(hashed, jnp.int32(16))
    return lax.shift_right_logical(hashed, jnp.int32(8)).astype(jnp.float32) / 16777216.0


def butterfly_sum(value, axis):
    count = lax.axis_size(axis)
    distance = 1
    while distance < count:
        partner = lax.ppermute(value, axis, [(i, i ^ distance) for i in range(count)])
        value = value + partner
        distance *= 2
    return value


def split_bf16(value):
    high = lax.reduce_precision(value, exponent_bits=8, mantissa_bits=7)
    low = (value - high).astype(jnp.bfloat16)
    return high.astype(jnp.bfloat16), low


def dot_f32(lhs, rhs, dims):
    return lax.dot_general(lhs, rhs, (dims, ((), ())), preferred_element_type=jnp.float32)


def per_device(
    byte_rows, cotangent, doc_ids, conv_weight, norm_gain, proj_weight, round_seed, step_count
):
    byte_block = byte_rows[0]
    upstream = cotangent[0]
    doc_block = doc_ids[0]
    length = byte_block.shape[0]
    row_width = byte_block.shape[1]
    patches = length // STRIDE
    half = STRIDE * row_width
    panel_rows = proj_weight.shape[0]
    next_bytes, next_up, next_docs = shifted(
        (byte_block[:STRIDE], upstream[:STRIDE], doc_block[:STRIDE]), "seq", -1
    )
    bytes_lo = byte_block.reshape(patches, half)
    bytes_hi = jnp.concatenate([bytes_lo[1:], next_bytes.reshape(1, half)], 0)
    up_lo = upstream.reshape(patches, half)
    up_hi = jnp.concatenate([up_lo[1:], next_up.reshape(1, half)], 0)
    docs_lo = doc_block.reshape(patches, STRIDE)
    docs_hi = jnp.concatenate([docs_lo[1:], next_docs.reshape(1, STRIDE)], 0)
    is_last = lax.axis_index("seq") == lax.axis_size("seq") - 1
    patch_ids = lax.broadcasted_iota(jnp.int32, (patches, STRIDE), 0)
    spilled = is_last & (patch_ids == patches - 1)
    keep_lo = docs_lo == docs_lo[:, :1]
    keep_hi = (docs_hi == docs_lo[:, :1]) & jnp.logical_not(spilled)

    def spread(keep):
        return jnp.broadcast_to(keep[:, :, None], (patches, STRIDE, row_width)).reshape(
            patches, half
        )

    keep_lo_f = spread(keep_lo.astype(jnp.float32))
    keep_hi_f = spread(keep_hi.astype(jnp.float32))
    win_lo = bytes_lo * keep_lo_f.astype(jnp.bfloat16)
    win_hi = bytes_hi * keep_hi_f.astype(jnp.bfloat16)

    tile_rows = lax.broadcasted_iota(jnp.int32, (CG, row_width), 0)
    tile_cols = lax.broadcasted_iota(jnp.int32, (CG, row_width), 1)
    tiler = (tile_cols % CG == tile_rows).astype(jnp.bfloat16)
    tiled = dot_f32(conv_weight.reshape(KERNEL * row_width, CG), tiler, ((1,), (0,)))
    block_rows = lax.broadcasted_iota(jnp.int32, (half, row_width), 0)
    block_cols = lax.broadcasted_iota(jnp.int32, (half, row_width), 1)
    on_block = (block_rows % row_width) // CG == block_cols // CG
    dense_weight = tiled.reshape(2, half, row_width)
    weight_lo = jnp.where(on_block, dense_weight[0], 0.0).astype(jnp.bfloat16)
    weight_hi = jnp.where(on_block, dense_weight[1], 0.0).astype(jnp.bfloat16)

    hidden = dot_f32(win_lo, weight_lo, ((1,), (0,))) + dot_f32(win_hi, weight_hi, ((1,), (0,)))
    factor = lax.rsqrt(jnp.mean(hidden * hidden, axis=-1, keepdims=True) + 1e-06)
    normed = (hidden * factor * norm_gain).astype(jnp.bfloat16)

    full_proj = lax.all_gather(proj_weight, "fsdp", axis=0, tiled=True)
    proj_lo = full_proj[:half]
    proj_hi = full_proj[half:]
    pre_lo = dot_f32(normed, proj_lo, ((1,), (1,)))
    pre_hi = dot_f32(normed, proj_hi, ((1,), (1,)))
    grad_pre_lo = (up_lo.astype(jnp.float32) * keep_lo_f * gelu_grad(pre_lo)).astype(jnp.bfloat16)
    grad_pre_hi = (up_hi.astype(jnp.float32) * keep_hi_f * gelu_grad(pre_hi)).astype(jnp.bfloat16)

    grad_pre = jnp.concatenate([grad_pre_lo, grad_pre_hi], 1)
    proj_part = dot_f32(grad_pre, normed, ((0,), (0,)))
    panel_part = lax.psum_scatter(proj_part, "fsdp", scatter_dimension=0, tiled=True)

    grad_norm = dot_f32(grad_pre_lo, proj_lo, ((1,), (0,))) + dot_f32(
        grad_pre_hi, proj_hi, ((1,), (0,))
    )
    gain_part = jnp.sum(grad_norm * hidden * factor, axis=0)
    gained = norm_gain * grad_norm
    grad_hidden = factor * gained - hidden * factor * factor * factor * jnp.mean(
        gained * hidden, axis=-1, keepdims=True
    )
    gh_high, gh_low = split_bf16(grad_hidden)

    def window_grad(window):
        full = dot_f32(window, gh_high, ((0,), (0,))) + dot_f32(window, gh_low, ((0,), (0,)))
        diagonal = lax.dot_general(
            jnp.where(on_block, full, 0.0),
            tiler.astype(jnp.float32),
            (((1,), (1,)), ((), ())),
            precision=lax.Precision.HIGHEST,
            preferred_element_type=jnp.float32,
        )
        return diagonal.reshape(STRIDE, GROUPS, CG, CG)

    conv_part = jnp.concatenate([window_grad(win_lo), window_grad(win_hi)], 0)

    def back_taps(weight, keep_f):
        taps = dot_f32(gh_high, weight, ((1,), (1,))) + dot_f32(gh_low, weight, ((1,), (1,)))
        return (taps * keep_f).reshape(length, row_width)

    back_lower = back_taps(weight_lo, keep_lo_f)
    back_upper = back_taps(weight_hi, keep_hi_f)
    incoming = shifted(back_upper[length - STRIDE :], "seq", 1)
    back_rows = back_lower + jnp.concatenate([incoming, back_upper[: length - STRIDE]], 0)
    grad_bytes = (upstream.astype(jnp.float32) + back_rows)[None]

    conv_size = conv_part.size
    small = jnp.concatenate([conv_part.reshape(-1), gain_part]).reshape(-1, row_width)
    joined = butterfly_sum(jnp.concatenate([panel_part, butterfly_sum(small, "fsdp")], 0), "seq")
    proj_sum = joined[:panel_rows]
    small_sum = joined[panel_rows:].reshape(-1)
    conv_sum = small_sum[:conv_size].reshape(conv_part.shape)
    gain_sum = small_sum[conv_size:]

    total_patches = patches * lax.axis_size("seq") * lax.axis_size("fsdp")
    grad_scale = 1.0 / math.sqrt(total_patches)
    first_panel = lax.axis_index("fsdp") * jnp.int32(panel_rows)
    row_index = first_panel + jnp.arange(panel_rows, dtype=jnp.int32)
    flat_index = (
        row_index[:, None] * jnp.int32(row_width) + jnp.arange(row_width, dtype=jnp.int32)[None, :]
    )
    dither_noise = mix_bits(flat_index, round_seed[0], step_count[0])
    grad_proj = proj_sum * grad_scale + QUANT * (dither_noise - 0.5)
    return (grad_bytes, grad_proj, conv_sum * grad_scale, gain_sum * grad_scale)


def solution(mesh):
    in_specs = (
        P("fsdp", "seq", None),
        P("fsdp", "seq", None),
        P("fsdp", "seq"),
        P(),
        P(),
        P("fsdp", None),
        P(),
        P(),
    )
    out_specs = (P("fsdp", "seq", None), P("fsdp", None), P(), P())
    return jax.shard_map(
        per_device, mesh=mesh, in_specs=in_specs, out_specs=out_specs, check_vma=False
    )
```

```python
import math

import jax
import jax.numpy as jnp
from jax import lax
from jax.sharding import PartitionSpec as P

GROUPS = 32
KERNEL = 8
STRIDE = 4
CG = 16


GELU_A = 0.7978845608028654
GELU_B = 0.044715
QUANT = 0.25


def shifted(value, axis, steps):
    count = lax.axis_size(axis)
    initial, last = (max(0, -steps), min(count, count - steps))
    return lax.ppermute(value, axis, [(source, source + steps) for source in range(initial, last)])


def gelu_grad(values):
    tangent = jnp.tanh(GELU_A * (values + GELU_B * values * values * values))
    return 0.5 * (1.0 + tangent) + 0.5 * values * (1.0 - tangent * tangent) * GELU_A * (
        1.0 + 3.0 * GELU_B * values * values
    )


def mix_bits(flat_index, seed_value, step_value):
    hashed = (
        flat_index * jnp.int32(-1640531535)
        + seed_value * jnp.int32(-2048144777)
        + step_value * jnp.int32(-1028477379)
    )
    hashed = hashed ^ lax.shift_right_logical(hashed, jnp.int32(16))
    hashed = hashed * jnp.int32(2146121005)
    hashed = hashed ^ lax.shift_right_logical(hashed, jnp.int32(15))
    hashed = hashed * jnp.int32(-2073254261)
    hashed = hashed ^ lax.shift_right_logical(hashed, jnp.int32(16))
    return lax.shift_right_logical(hashed, jnp.int32(8)).astype(jnp.float32) / 16777216.0


def butterfly_sum(value, axis):
    count = lax.axis_size(axis)
    distance = 1
    while distance < count:
        partner = lax.ppermute(value, axis, [(i, i ^ distance) for i in range(count)])
        value = value + partner
        distance *= 2
    return value


def split_bf16(value):
    high = lax.reduce_precision(value, exponent_bits=8, mantissa_bits=7)
    low = (value - high).astype(jnp.bfloat16)
    return high.astype(jnp.bfloat16), low


def dot_f32(lhs, rhs, dims):
    return lax.dot_general(lhs, rhs, (dims, ((), ())), preferred_element_type=jnp.float32)


def per_device(
    byte_rows, cotangent, doc_ids, conv_weight, norm_gain, proj_weight, round_seed, step_count
):
    byte_block = byte_rows[0]
    upstream = cotangent[0]
    doc_block = doc_ids[0]
    length = byte_block.shape[0]
    row_width = byte_block.shape[1]
    patches = length // STRIDE
    half = STRIDE * row_width
    panel_rows = proj_weight.shape[0]
    next_bytes, next_up, next_docs = shifted(
        (byte_block[:STRIDE], upstream[:STRIDE], doc_block[:STRIDE]), "seq", -1
    )
    bytes_lo = byte_block.reshape(patches, half)
    bytes_hi = jnp.concatenate([bytes_lo[1:], next_bytes.reshape(1, half)], 0)
    up_lo = upstream.reshape(patches, half)
    up_hi = jnp.concatenate([up_lo[1:], next_up.reshape(1, half)], 0)
    docs_lo = doc_block.reshape(patches, STRIDE)
    docs_hi = jnp.concatenate([docs_lo[1:], next_docs.reshape(1, STRIDE)], 0)
    is_last = lax.axis_index("seq") == lax.axis_size("seq") - 1
    patch_ids = lax.broadcasted_iota(jnp.int32, (patches, STRIDE), 0)
    spilled = is_last & (patch_ids == patches - 1)
    keep_lo = docs_lo == docs_lo[:, :1]
    keep_hi = (docs_hi == docs_lo[:, :1]) & jnp.logical_not(spilled)

    def spread(keep):
        return jnp.broadcast_to(keep[:, :, None], (patches, STRIDE, row_width)).reshape(
            patches, half
        )

    keep_lo_f = spread(keep_lo.astype(jnp.float32))
    keep_hi_f = spread(keep_hi.astype(jnp.float32))
    win_lo = bytes_lo * keep_lo_f.astype(jnp.bfloat16)
    win_hi = bytes_hi * keep_hi_f.astype(jnp.bfloat16)

    tile_rows = lax.broadcasted_iota(jnp.int32, (CG, row_width), 0)
    tile_cols = lax.broadcasted_iota(jnp.int32, (CG, row_width), 1)
    tiler = (tile_cols % CG == tile_rows).astype(jnp.bfloat16)
    tiled = dot_f32(conv_weight.reshape(KERNEL * row_width, CG), tiler, ((1,), (0,)))
    block_rows = lax.broadcasted_iota(jnp.int32, (half, row_width), 0)
    block_cols = lax.broadcasted_iota(jnp.int32, (half, row_width), 1)
    on_block = (block_rows % row_width) // CG == block_cols // CG
    dense_weight = tiled.reshape(2, half, row_width)
    weight_lo = jnp.where(on_block, dense_weight[0], 0.0).astype(jnp.bfloat16)
    weight_hi = jnp.where(on_block, dense_weight[1], 0.0).astype(jnp.bfloat16)

    hidden = dot_f32(win_lo, weight_lo, ((1,), (0,))) + dot_f32(win_hi, weight_hi, ((1,), (0,)))
    factor = lax.rsqrt(jnp.mean(hidden * hidden, axis=-1, keepdims=True) + 1e-06)
    normed = (hidden * factor * norm_gain).astype(jnp.bfloat16)

    full_proj = lax.all_gather(proj_weight, "fsdp", axis=0, tiled=True)
    proj_lo = full_proj[:half]
    proj_hi = full_proj[half:]
    pre_lo = dot_f32(normed, proj_lo, ((1,), (1,)))
    pre_hi = dot_f32(normed, proj_hi, ((1,), (1,)))
    grad_pre_lo = (up_lo.astype(jnp.float32) * keep_lo_f * gelu_grad(pre_lo)).astype(jnp.bfloat16)
    grad_pre_hi = (up_hi.astype(jnp.float32) * keep_hi_f * gelu_grad(pre_hi)).astype(jnp.bfloat16)

    grad_pre = jnp.concatenate([grad_pre_lo, grad_pre_hi], 1)
    proj_part = dot_f32(grad_pre, normed, ((0,), (0,)))
    panel_part = lax.psum_scatter(proj_part, "fsdp", scatter_dimension=0, tiled=True)

    grad_norm = dot_f32(grad_pre_lo, proj_lo, ((1,), (0,))) + dot_f32(
        grad_pre_hi, proj_hi, ((1,), (0,))
    )
    gain_part = jnp.sum(grad_norm * hidden * factor, axis=0)
    gained = norm_gain * grad_norm
    grad_hidden = factor * gained - hidden * factor * factor * factor * jnp.mean(
        gained * hidden, axis=-1, keepdims=True
    )
    gh_high, gh_low = split_bf16(grad_hidden)

    def window_grad(window):
        full = dot_f32(window, gh_high, ((0,), (0,))) + dot_f32(window, gh_low, ((0,), (0,)))
        diagonal = lax.dot_general(
            jnp.where(on_block, full, 0.0),
            tiler.astype(jnp.float32),
            (((1,), (1,)), ((), ())),
            precision=lax.Precision.HIGHEST,
            preferred_element_type=jnp.float32,
        )
        return diagonal.reshape(STRIDE, GROUPS, CG, CG)

    conv_part = jnp.concatenate([window_grad(win_lo), window_grad(win_hi)], 0)

    def back_taps(weight, keep_f):
        taps = dot_f32(gh_high, weight, ((1,), (1,))) + dot_f32(gh_low, weight, ((1,), (1,)))
        return (taps * keep_f).reshape(length, row_width)

    back_lower = back_taps(weight_lo, keep_lo_f)
    back_upper = back_taps(weight_hi, keep_hi_f)
    incoming = shifted(back_upper[length - STRIDE :], "seq", 1)
    back_rows = back_lower + jnp.concatenate([incoming, back_upper[: length - STRIDE]], 0)
    grad_bytes = (upstream.astype(jnp.float32) + back_rows)[None]

    conv_size = conv_part.size
    small = jnp.concatenate([conv_part.reshape(-1), gain_part]).reshape(-1, row_width)
    small_sum = butterfly_sum(butterfly_sum(small, "seq"), "fsdp").reshape(-1)
    proj_sum = butterfly_sum(panel_part, "seq")
    conv_sum = small_sum[:conv_size].reshape(conv_part.shape)
    gain_sum = small_sum[conv_size:]

    total_patches = patches * lax.axis_size("seq") * lax.axis_size("fsdp")
    grad_scale = 1.0 / math.sqrt(total_patches)
    first_panel = lax.axis_index("fsdp") * jnp.int32(panel_rows)
    row_index = first_panel + jnp.arange(panel_rows, dtype=jnp.int32)
    flat_index = (
        row_index[:, None] * jnp.int32(row_width) + jnp.arange(row_width, dtype=jnp.int32)[None, :]
    )
    dither_noise = mix_bits(flat_index, round_seed[0], step_count[0])
    grad_proj = proj_sum * grad_scale + QUANT * (dither_noise - 0.5)
    return (grad_bytes, grad_proj, conv_sum * grad_scale, gain_sum * grad_scale)


def solution(mesh):
    in_specs = (
        P("fsdp", "seq", None),
        P("fsdp", "seq", None),
        P("fsdp", "seq"),
        P(),
        P(),
        P("fsdp", None),
        P(),
        P(),
    )
    out_specs = (P("fsdp", "seq", None), P("fsdp", None), P(), P())
    return jax.shard_map(
        per_device, mesh=mesh, in_specs=in_specs, out_specs=out_specs, check_vma=False
    )
```

```python
import math

import jax
import jax.numpy as jnp
from jax import lax
from jax.sharding import PartitionSpec as P

GROUPS = 32
KERNEL = 8
STRIDE = 4
CG = 16


GELU_A = 0.7978845608028654
GELU_B = 0.044715
QUANT = 0.25


def shifted(value, axis, steps):
    count = lax.axis_size(axis)
    initial, last = (max(0, -steps), min(count, count - steps))
    return lax.ppermute(value, axis, [(source, source + steps) for source in range(initial, last)])


def gelu_grad(values):
    tangent = jnp.tanh(GELU_A * (values + GELU_B * values * values * values))
    return 0.5 * (1.0 + tangent) + 0.5 * values * (1.0 - tangent * tangent) * GELU_A * (
        1.0 + 3.0 * GELU_B * values * values
    )


def mix_bits(flat_index, seed_value, step_value):
    hashed = (
        flat_index * jnp.int32(-1640531535)
        + seed_value * jnp.int32(-2048144777)
        + step_value * jnp.int32(-1028477379)
    )
    hashed = hashed ^ lax.shift_right_logical(hashed, jnp.int32(16))
    hashed = hashed * jnp.int32(2146121005)
    hashed = hashed ^ lax.shift_right_logical(hashed, jnp.int32(15))
    hashed = hashed * jnp.int32(-2073254261)
    hashed = hashed ^ lax.shift_right_logical(hashed, jnp.int32(16))
    return lax.shift_right_logical(hashed, jnp.int32(8)).astype(jnp.float32) / 16777216.0


def butterfly_sum(value, axis):
    count = lax.axis_size(axis)
    distance = 1
    while distance < count:
        partner = lax.ppermute(value, axis, [(i, i ^ distance) for i in range(count)])
        value = value + partner
        distance *= 2
    return value


def split_bf16(value):
    high = lax.reduce_precision(value, exponent_bits=8, mantissa_bits=7)
    low = (value - high).astype(jnp.bfloat16)
    return high.astype(jnp.bfloat16), low


def dot_f32(lhs, rhs, dims):
    return lax.dot_general(lhs, rhs, (dims, ((), ())), preferred_element_type=jnp.float32)


def per_device(
    byte_rows, cotangent, doc_ids, conv_weight, norm_gain, proj_weight, round_seed, step_count
):
    byte_block = byte_rows[0]
    upstream = cotangent[0]
    doc_block = doc_ids[0]
    length = byte_block.shape[0]
    row_width = byte_block.shape[1]
    patches = length // STRIDE
    half = STRIDE * row_width
    panel_rows = proj_weight.shape[0]
    next_bytes, next_up, next_docs = shifted(
        (byte_block[:STRIDE], upstream[:STRIDE], doc_block[:STRIDE]), "seq", -1
    )
    bytes_lo = byte_block.reshape(patches, half)
    bytes_hi = jnp.concatenate([bytes_lo[1:], next_bytes.reshape(1, half)], 0)
    up_lo = upstream.reshape(patches, half)
    up_hi = jnp.concatenate([up_lo[1:], next_up.reshape(1, half)], 0)
    docs_lo = doc_block.reshape(patches, STRIDE)
    docs_hi = jnp.concatenate([docs_lo[1:], next_docs.reshape(1, STRIDE)], 0)
    is_last = lax.axis_index("seq") == lax.axis_size("seq") - 1
    patch_ids = lax.broadcasted_iota(jnp.int32, (patches, STRIDE), 0)
    spilled = is_last & (patch_ids == patches - 1)
    keep_lo = docs_lo == docs_lo[:, :1]
    keep_hi = (docs_hi == docs_lo[:, :1]) & jnp.logical_not(spilled)

    def spread(keep):
        return jnp.broadcast_to(keep[:, :, None], (patches, STRIDE, row_width)).reshape(
            patches, half
        )

    keep_lo_f = spread(keep_lo.astype(jnp.float32))
    keep_hi_f = spread(keep_hi.astype(jnp.float32))
    win_lo = bytes_lo * keep_lo_f.astype(jnp.bfloat16)
    win_hi = bytes_hi * keep_hi_f.astype(jnp.bfloat16)

    tile_rows = lax.broadcasted_iota(jnp.int32, (CG, row_width), 0)
    tile_cols = lax.broadcasted_iota(jnp.int32, (CG, row_width), 1)
    tiler = (tile_cols % CG == tile_rows).astype(jnp.bfloat16)
    tiled = dot_f32(conv_weight.reshape(KERNEL * row_width, CG), tiler, ((1,), (0,)))
    block_rows = lax.broadcasted_iota(jnp.int32, (half, row_width), 0)
    block_cols = lax.broadcasted_iota(jnp.int32, (half, row_width), 1)
    on_block = (block_rows % row_width) // CG == block_cols // CG
    dense_weight = tiled.reshape(2, half, row_width)
    weight_lo = jnp.where(on_block, dense_weight[0], 0.0).astype(jnp.bfloat16)
    weight_hi = jnp.where(on_block, dense_weight[1], 0.0).astype(jnp.bfloat16)

    hidden = dot_f32(win_lo, weight_lo, ((1,), (0,))) + dot_f32(win_hi, weight_hi, ((1,), (0,)))
    factor = lax.rsqrt(jnp.mean(hidden * hidden, axis=-1, keepdims=True) + 1e-06)
    normed = (hidden * factor * norm_gain).astype(jnp.bfloat16)

    full_proj = lax.all_gather(proj_weight, "fsdp", axis=0, tiled=True)
    proj_lo = full_proj[:half]
    proj_hi = full_proj[half:]
    pre_lo = dot_f32(normed, proj_lo, ((1,), (1,)))
    pre_hi = dot_f32(normed, proj_hi, ((1,), (1,)))
    grad_pre_lo = (up_lo.astype(jnp.float32) * keep_lo_f * gelu_grad(pre_lo)).astype(jnp.bfloat16)
    grad_pre_hi = (up_hi.astype(jnp.float32) * keep_hi_f * gelu_grad(pre_hi)).astype(jnp.bfloat16)

    grad_pre = jnp.concatenate([grad_pre_lo, grad_pre_hi], 1)
    proj_part = dot_f32(grad_pre, normed, ((0,), (0,)))
    panel_part = lax.psum_scatter(proj_part, "fsdp", scatter_dimension=0, tiled=True)

    grad_norm = dot_f32(grad_pre_lo, proj_lo, ((1,), (0,))) + dot_f32(
        grad_pre_hi, proj_hi, ((1,), (0,))
    )
    gain_part = jnp.sum(grad_norm * hidden * factor, axis=0)
    gained = norm_gain * grad_norm
    grad_hidden = factor * gained - hidden * factor * factor * factor * jnp.mean(
        gained * hidden, axis=-1, keepdims=True
    )
    gh_high, gh_low = split_bf16(grad_hidden)

    def window_grad(window):
        full = dot_f32(window, gh_high, ((0,), (0,))) + dot_f32(window, gh_low, ((0,), (0,)))
        diagonal = lax.dot_general(
            jnp.where(on_block, full, 0.0),
            tiler.astype(jnp.float32),
            (((1,), (1,)), ((), ())),
            precision=lax.Precision.HIGHEST,
            preferred_element_type=jnp.float32,
        )
        return diagonal.reshape(STRIDE, GROUPS, CG, CG)

    conv_part = jnp.concatenate([window_grad(win_lo), window_grad(win_hi)], 0)

    def back_taps(weight, keep_f):
        taps = dot_f32(gh_high, weight, ((1,), (1,))) + dot_f32(gh_low, weight, ((1,), (1,)))
        return (taps * keep_f).reshape(length, row_width)

    back_lower = back_taps(weight_lo, keep_lo_f)
    back_upper = back_taps(weight_hi, keep_hi_f)
    incoming = shifted(back_upper[length - STRIDE :], "seq", 1)
    back_rows = back_lower + jnp.concatenate([incoming, back_upper[: length - STRIDE]], 0)
    grad_bytes = (upstream.astype(jnp.float32) + back_rows)[None]

    conv_size = conv_part.size
    small = jnp.concatenate([conv_part.reshape(-1), gain_part]).reshape(-1, row_width)
    small = butterfly_sum(small, "seq")
    panel_part, small, grad_bytes = lax.optimization_barrier((panel_part, small, grad_bytes))
    small_sum = butterfly_sum(small, "fsdp").reshape(-1)
    proj_sum = butterfly_sum(panel_part, "seq")
    conv_sum = small_sum[:conv_size].reshape(conv_part.shape)
    gain_sum = small_sum[conv_size:]

    total_patches = patches * lax.axis_size("seq") * lax.axis_size("fsdp")
    grad_scale = 1.0 / math.sqrt(total_patches)
    first_panel = lax.axis_index("fsdp") * jnp.int32(panel_rows)
    row_index = first_panel + jnp.arange(panel_rows, dtype=jnp.int32)
    flat_index = (
        row_index[:, None] * jnp.int32(row_width) + jnp.arange(row_width, dtype=jnp.int32)[None, :]
    )
    dither_noise = mix_bits(flat_index, round_seed[0], step_count[0])
    grad_proj = proj_sum * grad_scale + QUANT * (dither_noise - 0.5)
    return (grad_bytes, grad_proj, conv_sum * grad_scale, gain_sum * grad_scale)


def solution(mesh):
    in_specs = (
        P("fsdp", "seq", None),
        P("fsdp", "seq", None),
        P("fsdp", "seq"),
        P(),
        P(),
        P("fsdp", None),
        P(),
        P(),
    )
    out_specs = (P("fsdp", "seq", None), P("fsdp", None), P(), P())
    return jax.shard_map(
        per_device, mesh=mesh, in_specs=in_specs, out_specs=out_specs, check_vma=False
    )
```

```python
import math

import jax
import jax.numpy as jnp
from jax import lax
from jax.sharding import PartitionSpec as P

GROUPS = 32
KERNEL = 8
STRIDE = 4
CG = 16


GELU_A = 0.7978845608028654
GELU_B = 0.044715
QUANT = 0.25


def shifted(value, axis, steps):
    count = lax.axis_size(axis)
    initial, last = (max(0, -steps), min(count, count - steps))
    return lax.ppermute(value, axis, [(source, source + steps) for source in range(initial, last)])


def gelu_grad(values):
    tangent = jnp.tanh(GELU_A * (values + GELU_B * values * values * values))
    return 0.5 * (1.0 + tangent) + 0.5 * values * (1.0 - tangent * tangent) * GELU_A * (
        1.0 + 3.0 * GELU_B * values * values
    )


def mix_bits(flat_index, seed_value, step_value):
    hashed = (
        flat_index * jnp.int32(-1640531535)
        + seed_value * jnp.int32(-2048144777)
        + step_value * jnp.int32(-1028477379)
    )
    hashed = hashed ^ lax.shift_right_logical(hashed, jnp.int32(16))
    hashed = hashed * jnp.int32(2146121005)
    hashed = hashed ^ lax.shift_right_logical(hashed, jnp.int32(15))
    hashed = hashed * jnp.int32(-2073254261)
    hashed = hashed ^ lax.shift_right_logical(hashed, jnp.int32(16))
    return lax.shift_right_logical(hashed, jnp.int32(8)).astype(jnp.float32) / 16777216.0


def butterfly_sum(value, axis, first=0, last=None):
    count = lax.axis_size(axis)
    last = count.bit_length() - 1 if last is None else last
    for level in range(first, last):
        distance = 1 << level
        partner = lax.ppermute(value, axis, [(i, i ^ distance) for i in range(count)])
        value = value + partner
    return value


def split_bf16(value):
    high = lax.reduce_precision(value, exponent_bits=8, mantissa_bits=7)
    low = (value - high).astype(jnp.bfloat16)
    return high.astype(jnp.bfloat16), low


def dot_f32(lhs, rhs, dims):
    return lax.dot_general(lhs, rhs, (dims, ((), ())), preferred_element_type=jnp.float32)


def per_device(
    byte_rows, cotangent, doc_ids, conv_weight, norm_gain, proj_weight, round_seed, step_count
):
    byte_block = byte_rows[0]
    upstream = cotangent[0]
    doc_block = doc_ids[0]
    length = byte_block.shape[0]
    row_width = byte_block.shape[1]
    patches = length // STRIDE
    half = STRIDE * row_width
    panel_rows = proj_weight.shape[0]
    next_bytes, next_up, next_docs = shifted(
        (byte_block[:STRIDE], upstream[:STRIDE], doc_block[:STRIDE]), "seq", -1
    )
    bytes_lo = byte_block.reshape(patches, half)
    bytes_hi = jnp.concatenate([bytes_lo[1:], next_bytes.reshape(1, half)], 0)
    up_lo = upstream.reshape(patches, half)
    up_hi = jnp.concatenate([up_lo[1:], next_up.reshape(1, half)], 0)
    docs_lo = doc_block.reshape(patches, STRIDE)
    docs_hi = jnp.concatenate([docs_lo[1:], next_docs.reshape(1, STRIDE)], 0)
    is_last = lax.axis_index("seq") == lax.axis_size("seq") - 1
    patch_ids = lax.broadcasted_iota(jnp.int32, (patches, STRIDE), 0)
    spilled = is_last & (patch_ids == patches - 1)
    keep_lo = docs_lo == docs_lo[:, :1]
    keep_hi = (docs_hi == docs_lo[:, :1]) & jnp.logical_not(spilled)

    def spread(keep):
        return jnp.broadcast_to(keep[:, :, None], (patches, STRIDE, row_width)).reshape(
            patches, half
        )

    keep_lo_f = spread(keep_lo.astype(jnp.float32))
    keep_hi_f = spread(keep_hi.astype(jnp.float32))
    win_lo = bytes_lo * keep_lo_f.astype(jnp.bfloat16)
    win_hi = bytes_hi * keep_hi_f.astype(jnp.bfloat16)

    tile_rows = lax.broadcasted_iota(jnp.int32, (CG, row_width), 0)
    tile_cols = lax.broadcasted_iota(jnp.int32, (CG, row_width), 1)
    tiler = (tile_cols % CG == tile_rows).astype(jnp.bfloat16)
    tiled = dot_f32(conv_weight.reshape(KERNEL * row_width, CG), tiler, ((1,), (0,)))
    block_rows = lax.broadcasted_iota(jnp.int32, (half, row_width), 0)
    block_cols = lax.broadcasted_iota(jnp.int32, (half, row_width), 1)
    on_block = (block_rows % row_width) // CG == block_cols // CG
    dense_weight = tiled.reshape(2, half, row_width)
    weight_lo = jnp.where(on_block, dense_weight[0], 0.0).astype(jnp.bfloat16)
    weight_hi = jnp.where(on_block, dense_weight[1], 0.0).astype(jnp.bfloat16)

    hidden = dot_f32(win_lo, weight_lo, ((1,), (0,))) + dot_f32(win_hi, weight_hi, ((1,), (0,)))
    factor = lax.rsqrt(jnp.mean(hidden * hidden, axis=-1, keepdims=True) + 1e-06)
    normed = (hidden * factor * norm_gain).astype(jnp.bfloat16)

    full_proj = lax.all_gather(proj_weight, "fsdp", axis=0, tiled=True)
    proj_lo = full_proj[:half]
    proj_hi = full_proj[half:]
    pre_lo = dot_f32(normed, proj_lo, ((1,), (1,)))
    pre_hi = dot_f32(normed, proj_hi, ((1,), (1,)))
    grad_pre_lo = (up_lo.astype(jnp.float32) * keep_lo_f * gelu_grad(pre_lo)).astype(jnp.bfloat16)
    grad_pre_hi = (up_hi.astype(jnp.float32) * keep_hi_f * gelu_grad(pre_hi)).astype(jnp.bfloat16)

    grad_pre = jnp.concatenate([grad_pre_lo, grad_pre_hi], 1)
    proj_part = dot_f32(grad_pre, normed, ((0,), (0,)))
    panel_part = lax.psum_scatter(proj_part, "fsdp", scatter_dimension=0, tiled=True)

    grad_norm = dot_f32(grad_pre_lo, proj_lo, ((1,), (0,))) + dot_f32(
        grad_pre_hi, proj_hi, ((1,), (0,))
    )
    gain_part = jnp.sum(grad_norm * hidden * factor, axis=0)
    gained = norm_gain * grad_norm
    grad_hidden = factor * gained - hidden * factor * factor * factor * jnp.mean(
        gained * hidden, axis=-1, keepdims=True
    )
    gh_high, gh_low = split_bf16(grad_hidden)

    def window_grad(window):
        full = dot_f32(window, gh_high, ((0,), (0,))) + dot_f32(window, gh_low, ((0,), (0,)))
        diagonal = lax.dot_general(
            jnp.where(on_block, full, 0.0),
            tiler.astype(jnp.float32),
            (((1,), (1,)), ((), ())),
            precision=lax.Precision.HIGHEST,
            preferred_element_type=jnp.float32,
        )
        return diagonal.reshape(STRIDE, GROUPS, CG, CG)

    conv_part = jnp.concatenate([window_grad(win_lo), window_grad(win_hi)], 0)

    def back_taps(weight, keep_f):
        taps = dot_f32(gh_high, weight, ((1,), (1,))) + dot_f32(gh_low, weight, ((1,), (1,)))
        return (taps * keep_f).reshape(length, row_width)

    back_lower = back_taps(weight_lo, keep_lo_f)
    back_upper = back_taps(weight_hi, keep_hi_f)
    incoming = shifted(back_upper[length - STRIDE :], "seq", 1)
    back_rows = back_lower + jnp.concatenate([incoming, back_upper[: length - STRIDE]], 0)
    grad_bytes = (upstream.astype(jnp.float32) + back_rows)[None]

    conv_size = conv_part.size
    small = jnp.concatenate([conv_part.reshape(-1), gain_part]).reshape(-1, row_width)
    small = butterfly_sum(small, "seq")
    panel_part, small, grad_bytes = lax.optimization_barrier((panel_part, small, grad_bytes))
    for level in range(lax.axis_size("seq").bit_length() - 1):
        panel_part = butterfly_sum(panel_part, "seq", level, level + 1)
        small = butterfly_sum(small, "fsdp", level, level + 1)
        panel_part, small = lax.optimization_barrier((panel_part, small))
    proj_sum = panel_part
    small_sum = small.reshape(-1)
    conv_sum = small_sum[:conv_size].reshape(conv_part.shape)
    gain_sum = small_sum[conv_size:]

    total_patches = patches * lax.axis_size("seq") * lax.axis_size("fsdp")
    grad_scale = 1.0 / math.sqrt(total_patches)
    first_panel = lax.axis_index("fsdp") * jnp.int32(panel_rows)
    row_index = first_panel + jnp.arange(panel_rows, dtype=jnp.int32)
    flat_index = (
        row_index[:, None] * jnp.int32(row_width) + jnp.arange(row_width, dtype=jnp.int32)[None, :]
    )
    dither_noise = mix_bits(flat_index, round_seed[0], step_count[0])
    grad_proj = proj_sum * grad_scale + QUANT * (dither_noise - 0.5)
    return (grad_bytes, grad_proj, conv_sum * grad_scale, gain_sum * grad_scale)


def solution(mesh):
    in_specs = (
        P("fsdp", "seq", None),
        P("fsdp", "seq", None),
        P("fsdp", "seq"),
        P(),
        P(),
        P("fsdp", None),
        P(),
        P(),
    )
    out_specs = (P("fsdp", "seq", None), P("fsdp", None), P(), P())
    return jax.shard_map(
        per_device, mesh=mesh, in_specs=in_specs, out_specs=out_specs, check_vma=False
    )
```

```python
import math

import jax
import jax.numpy as jnp
from jax import lax
from jax.sharding import PartitionSpec as P

GROUPS = 32
KERNEL = 8
STRIDE = 4
CG = 16


GELU_A = 0.7978845608028654
GELU_B = 0.044715
QUANT = 0.25


def shifted(value, axis, steps):
    count = lax.axis_size(axis)
    initial, last = (max(0, -steps), min(count, count - steps))
    return lax.ppermute(value, axis, [(source, source + steps) for source in range(initial, last)])


def gelu_grad(values):
    tangent = jnp.tanh(GELU_A * (values + GELU_B * values * values * values))
    return 0.5 * (1.0 + tangent) + 0.5 * values * (1.0 - tangent * tangent) * GELU_A * (
        1.0 + 3.0 * GELU_B * values * values
    )


def mix_bits(flat_index, seed_value, step_value):
    hashed = (
        flat_index * jnp.int32(-1640531535)
        + seed_value * jnp.int32(-2048144777)
        + step_value * jnp.int32(-1028477379)
    )
    hashed = hashed ^ lax.shift_right_logical(hashed, jnp.int32(16))
    hashed = hashed * jnp.int32(2146121005)
    hashed = hashed ^ lax.shift_right_logical(hashed, jnp.int32(15))
    hashed = hashed * jnp.int32(-2073254261)
    hashed = hashed ^ lax.shift_right_logical(hashed, jnp.int32(16))
    return lax.shift_right_logical(hashed, jnp.int32(8)).astype(jnp.float32) / 16777216.0


def butterfly_sum(value, axis, first=0, last=None):
    count = lax.axis_size(axis)
    last = count.bit_length() - 1 if last is None else last
    for level in range(first, last):
        distance = 1 << level
        partner = lax.ppermute(value, axis, [(i, i ^ distance) for i in range(count)])
        value = value + partner
    return value


def split_bf16(value):
    high = lax.reduce_precision(value, exponent_bits=8, mantissa_bits=7)
    low = (value - high).astype(jnp.bfloat16)
    return high.astype(jnp.bfloat16), low


def dot_f32(lhs, rhs, dims):
    return lax.dot_general(lhs, rhs, (dims, ((), ())), preferred_element_type=jnp.float32)


def per_device(
    byte_rows, cotangent, doc_ids, conv_weight, norm_gain, proj_weight, round_seed, step_count
):
    byte_block = byte_rows[0]
    upstream = cotangent[0]
    doc_block = doc_ids[0]
    length = byte_block.shape[0]
    row_width = byte_block.shape[1]
    patches = length // STRIDE
    half = STRIDE * row_width
    panel_rows = proj_weight.shape[0]
    next_bytes, next_up, next_docs = shifted(
        (byte_block[:STRIDE], upstream[:STRIDE], doc_block[:STRIDE]), "seq", -1
    )
    bytes_lo = byte_block.reshape(patches, half)
    bytes_hi = jnp.concatenate([bytes_lo[1:], next_bytes.reshape(1, half)], 0)
    up_lo = upstream.reshape(patches, half)
    up_hi = jnp.concatenate([up_lo[1:], next_up.reshape(1, half)], 0)
    docs_lo = doc_block.reshape(patches, STRIDE)
    docs_hi = jnp.concatenate([docs_lo[1:], next_docs.reshape(1, STRIDE)], 0)
    is_last = lax.axis_index("seq") == lax.axis_size("seq") - 1
    patch_ids = lax.broadcasted_iota(jnp.int32, (patches, STRIDE), 0)
    spilled = is_last & (patch_ids == patches - 1)
    keep_lo = docs_lo == docs_lo[:, :1]
    keep_hi = (docs_hi == docs_lo[:, :1]) & jnp.logical_not(spilled)

    def spread(keep):
        return jnp.broadcast_to(keep[:, :, None], (patches, STRIDE, row_width)).reshape(
            patches, half
        )

    keep_lo_f = spread(keep_lo.astype(jnp.float32))
    keep_hi_f = spread(keep_hi.astype(jnp.float32))
    win_lo = bytes_lo * keep_lo_f.astype(jnp.bfloat16)
    win_hi = bytes_hi * keep_hi_f.astype(jnp.bfloat16)

    tile_rows = lax.broadcasted_iota(jnp.int32, (CG, row_width), 0)
    tile_cols = lax.broadcasted_iota(jnp.int32, (CG, row_width), 1)
    tiler = (tile_cols % CG == tile_rows).astype(jnp.bfloat16)
    tiled = dot_f32(conv_weight.reshape(KERNEL * row_width, CG), tiler, ((1,), (0,)))
    block_rows = lax.broadcasted_iota(jnp.int32, (half, row_width), 0)
    block_cols = lax.broadcasted_iota(jnp.int32, (half, row_width), 1)
    on_block = (block_rows % row_width) // CG == block_cols // CG
    dense_weight = tiled.reshape(2, half, row_width)
    weight_lo = jnp.where(on_block, dense_weight[0], 0.0).astype(jnp.bfloat16)
    weight_hi = jnp.where(on_block, dense_weight[1], 0.0).astype(jnp.bfloat16)

    hidden = dot_f32(win_lo, weight_lo, ((1,), (0,))) + dot_f32(win_hi, weight_hi, ((1,), (0,)))
    factor = lax.rsqrt(jnp.mean(hidden * hidden, axis=-1, keepdims=True) + 1e-06)
    normed = (hidden * factor * norm_gain).astype(jnp.bfloat16)

    full_proj = lax.all_gather(proj_weight, "fsdp", axis=0, tiled=True)
    proj_lo = full_proj[:half]
    proj_hi = full_proj[half:]
    pre_lo = dot_f32(normed, proj_lo, ((1,), (1,)))
    pre_hi = dot_f32(normed, proj_hi, ((1,), (1,)))
    grad_pre_lo = (up_lo.astype(jnp.float32) * keep_lo_f * gelu_grad(pre_lo)).astype(jnp.bfloat16)
    grad_pre_hi = (up_hi.astype(jnp.float32) * keep_hi_f * gelu_grad(pre_hi)).astype(jnp.bfloat16)

    grad_pre = jnp.concatenate([grad_pre_lo, grad_pre_hi], 1)
    proj_part = dot_f32(grad_pre, normed, ((0,), (0,)))
    panel_part = lax.psum_scatter(proj_part, "fsdp", scatter_dimension=0, tiled=True)

    grad_norm = dot_f32(grad_pre_lo, proj_lo, ((1,), (0,))) + dot_f32(
        grad_pre_hi, proj_hi, ((1,), (0,))
    )
    gain_part = jnp.sum(grad_norm * hidden * factor, axis=0)
    gained = norm_gain * grad_norm
    grad_hidden = factor * gained - hidden * factor * factor * factor * jnp.mean(
        gained * hidden, axis=-1, keepdims=True
    )
    gh_high, gh_low = split_bf16(grad_hidden)

    def window_grad(window):
        full = dot_f32(window, gh_high, ((0,), (0,))) + dot_f32(window, gh_low, ((0,), (0,)))
        return lax.dot_general(
            tiler.astype(jnp.float32),
            jnp.where(on_block, full, 0.0),
            (((1,), (1,)), ((), ())),
            precision=lax.Precision.HIGHEST,
            preferred_element_type=jnp.float32,
        )

    conv_part = jnp.concatenate([window_grad(win_lo), window_grad(win_hi)], 1)

    def back_taps(weight, keep_f):
        taps = dot_f32(gh_high, weight, ((1,), (1,))) + dot_f32(gh_low, weight, ((1,), (1,)))
        return (taps * keep_f).reshape(length, row_width)

    back_lower = back_taps(weight_lo, keep_lo_f)
    back_upper = back_taps(weight_hi, keep_hi_f)
    incoming = shifted(back_upper[length - STRIDE :], "seq", 1)
    back_rows = back_lower + jnp.concatenate([incoming, back_upper[: length - STRIDE]], 0)
    grad_bytes = (upstream.astype(jnp.float32) + back_rows)[None]

    gain_row = jnp.pad(gain_part[None, :], ((0, 0), (0, conv_part.shape[1] - row_width)))
    small = jnp.concatenate([conv_part, gain_row], 0)
    small = butterfly_sum(small, "seq")
    panel_part, small, grad_bytes = lax.optimization_barrier((panel_part, small, grad_bytes))
    for level in range(lax.axis_size("seq").bit_length() - 1):
        panel_part = butterfly_sum(panel_part, "seq", level, level + 1)
        small = butterfly_sum(small, "fsdp", level, level + 1)
        panel_part, small = lax.optimization_barrier((panel_part, small))
    proj_sum = panel_part
    conv_sum = small[:CG].T.reshape(KERNEL, GROUPS, CG, CG)
    gain_sum = small[CG, :row_width]

    total_patches = patches * lax.axis_size("seq") * lax.axis_size("fsdp")
    grad_scale = 1.0 / math.sqrt(total_patches)
    first_panel = lax.axis_index("fsdp") * jnp.int32(panel_rows)
    row_index = first_panel + jnp.arange(panel_rows, dtype=jnp.int32)
    flat_index = (
        row_index[:, None] * jnp.int32(row_width) + jnp.arange(row_width, dtype=jnp.int32)[None, :]
    )
    dither_noise = mix_bits(flat_index, round_seed[0], step_count[0])
    grad_proj = proj_sum * grad_scale + QUANT * (dither_noise - 0.5)
    return (grad_bytes, grad_proj, conv_sum * grad_scale, gain_sum * grad_scale)


def solution(mesh):
    in_specs = (
        P("fsdp", "seq", None),
        P("fsdp", "seq", None),
        P("fsdp", "seq"),
        P(),
        P(),
        P("fsdp", None),
        P(),
        P(),
    )
    out_specs = (P("fsdp", "seq", None), P("fsdp", None), P(), P())
    return jax.shard_map(
        per_device, mesh=mesh, in_specs=in_specs, out_specs=out_specs, check_vma=False
    )
```

```python
import math

import jax
import jax.numpy as jnp
from jax import lax
from jax.sharding import PartitionSpec as P

GROUPS = 32
KERNEL = 8
STRIDE = 4
CG = 16


GELU_A = 0.7978845608028654
GELU_B = 0.044715
QUANT = 0.25


def shifted(value, axis, steps):
    count = lax.axis_size(axis)
    initial, last = (max(0, -steps), min(count, count - steps))
    return lax.ppermute(value, axis, [(source, source + steps) for source in range(initial, last)])


def gelu_grad(values):
    tangent = jnp.tanh(GELU_A * (values + GELU_B * values * values * values))
    return 0.5 * (1.0 + tangent) + 0.5 * values * (1.0 - tangent * tangent) * GELU_A * (
        1.0 + 3.0 * GELU_B * values * values
    )


def mix_bits(flat_index, seed_value, step_value):
    hashed = (
        flat_index * jnp.int32(-1640531535)
        + seed_value * jnp.int32(-2048144777)
        + step_value * jnp.int32(-1028477379)
    )
    hashed = hashed ^ lax.shift_right_logical(hashed, jnp.int32(16))
    hashed = hashed * jnp.int32(2146121005)
    hashed = hashed ^ lax.shift_right_logical(hashed, jnp.int32(15))
    hashed = hashed * jnp.int32(-2073254261)
    hashed = hashed ^ lax.shift_right_logical(hashed, jnp.int32(16))
    return lax.shift_right_logical(hashed, jnp.int32(8)).astype(jnp.float32) / 16777216.0


def butterfly_sum(value, axis, first=0, last=None):
    count = lax.axis_size(axis)
    last = count.bit_length() - 1 if last is None else last
    for level in range(first, last):
        distance = 1 << level
        partner = lax.ppermute(value, axis, [(i, i ^ distance) for i in range(count)])
        value = value + partner
    return value


def split_bf16(value):
    high = lax.reduce_precision(value, exponent_bits=8, mantissa_bits=7)
    low = (value - high).astype(jnp.bfloat16)
    return high.astype(jnp.bfloat16), low


def dot_f32(lhs, rhs, dims):
    return lax.dot_general(lhs, rhs, (dims, ((), ())), preferred_element_type=jnp.float32)


def per_device(
    byte_rows, cotangent, doc_ids, conv_weight, norm_gain, proj_weight, round_seed, step_count
):
    byte_block = byte_rows[0]
    upstream = cotangent[0]
    doc_block = doc_ids[0]
    length = byte_block.shape[0]
    row_width = byte_block.shape[1]
    patches = length // STRIDE
    half = STRIDE * row_width
    panel_rows = proj_weight.shape[0]
    next_bytes, next_up, next_docs = shifted(
        (byte_block[:STRIDE], upstream[:STRIDE], doc_block[:STRIDE]), "seq", -1
    )
    bytes_lo = byte_block.reshape(patches, half)
    bytes_hi = jnp.concatenate([bytes_lo[1:], next_bytes.reshape(1, half)], 0)
    up_lo = upstream.reshape(patches, half)
    up_hi = jnp.concatenate([up_lo[1:], next_up.reshape(1, half)], 0)
    docs_lo = doc_block.reshape(patches, STRIDE)
    docs_hi = jnp.concatenate([docs_lo[1:], next_docs.reshape(1, STRIDE)], 0)
    is_last = lax.axis_index("seq") == lax.axis_size("seq") - 1
    patch_ids = lax.broadcasted_iota(jnp.int32, (patches, STRIDE), 0)
    spilled = is_last & (patch_ids == patches - 1)
    keep_lo = docs_lo == docs_lo[:, :1]
    keep_hi = (docs_hi == docs_lo[:, :1]) & jnp.logical_not(spilled)

    def spread(keep):
        return jnp.broadcast_to(keep[:, :, None], (patches, STRIDE, row_width)).reshape(
            patches, half
        )

    keep_lo_f = spread(keep_lo.astype(jnp.float32))
    keep_hi_f = spread(keep_hi.astype(jnp.float32))
    win_lo = bytes_lo * keep_lo_f.astype(jnp.bfloat16)
    win_hi = bytes_hi * keep_hi_f.astype(jnp.bfloat16)

    tile_rows = lax.broadcasted_iota(jnp.int32, (CG, row_width), 0)
    tile_cols = lax.broadcasted_iota(jnp.int32, (CG, row_width), 1)
    tiler = (tile_cols % CG == tile_rows).astype(jnp.bfloat16)
    tiled = dot_f32(conv_weight.reshape(KERNEL * row_width, CG), tiler, ((1,), (0,)))
    block_rows = lax.broadcasted_iota(jnp.int32, (half, row_width), 0)
    block_cols = lax.broadcasted_iota(jnp.int32, (half, row_width), 1)
    on_block = (block_rows % row_width) // CG == block_cols // CG
    dense_weight = tiled.reshape(2, half, row_width)
    weight_lo = jnp.where(on_block, dense_weight[0], 0.0).astype(jnp.bfloat16)
    weight_hi = jnp.where(on_block, dense_weight[1], 0.0).astype(jnp.bfloat16)

    hidden = dot_f32(win_lo, weight_lo, ((1,), (0,))) + dot_f32(win_hi, weight_hi, ((1,), (0,)))
    factor = lax.rsqrt(jnp.mean(hidden * hidden, axis=-1, keepdims=True) + 1e-06)
    normed = (hidden * factor * norm_gain).astype(jnp.bfloat16)

    full_proj = lax.all_gather(proj_weight, "fsdp", axis=0, tiled=True)
    proj_lo = full_proj[:half]
    proj_hi = full_proj[half:]
    pre_lo = dot_f32(normed, proj_lo, ((1,), (1,)))
    pre_hi = dot_f32(normed, proj_hi, ((1,), (1,)))
    grad_pre_lo = (up_lo.astype(jnp.float32) * keep_lo_f * gelu_grad(pre_lo)).astype(jnp.bfloat16)
    grad_pre_hi = (up_hi.astype(jnp.float32) * keep_hi_f * gelu_grad(pre_hi)).astype(jnp.bfloat16)

    grad_pre = jnp.concatenate([grad_pre_lo, grad_pre_hi], 1)
    proj_part = dot_f32(grad_pre, normed, ((0,), (0,)))
    panel_part = lax.psum_scatter(proj_part, "fsdp", scatter_dimension=0, tiled=True)

    grad_norm = dot_f32(grad_pre_lo, proj_lo, ((1,), (0,))) + dot_f32(
        grad_pre_hi, proj_hi, ((1,), (0,))
    )
    gain_part = jnp.sum(grad_norm * hidden * factor, axis=0)
    gained = norm_gain * grad_norm
    grad_hidden = factor * gained - hidden * factor * factor * factor * jnp.mean(
        gained * hidden, axis=-1, keepdims=True
    )
    gh_high, gh_low = split_bf16(grad_hidden)

    def window_grad(window):
        full = dot_f32(window, gh_high, ((0,), (0,))) + dot_f32(window, gh_low, ((0,), (0,)))
        diagonal = lax.dot_general(
            jnp.where(on_block, full, 0.0),
            tiler.astype(jnp.float32),
            (((1,), (1,)), ((), ())),
            precision=lax.Precision.HIGHEST,
            preferred_element_type=jnp.float32,
        )
        return diagonal.reshape(STRIDE, GROUPS, CG, CG)

    conv_part = jnp.concatenate([window_grad(win_lo), window_grad(win_hi)], 0)

    def back_taps(weight, keep_f):
        taps = dot_f32(gh_high, weight, ((1,), (1,))) + dot_f32(gh_low, weight, ((1,), (1,)))
        return (taps * keep_f).reshape(length, row_width)

    back_lower = back_taps(weight_lo, keep_lo_f)
    back_upper = back_taps(weight_hi, keep_hi_f)
    incoming = shifted(back_upper[length - STRIDE :], "seq", 1)
    back_rows = back_lower + jnp.concatenate([incoming, back_upper[: length - STRIDE]], 0)
    grad_bytes = (upstream.astype(jnp.float32) + back_rows)[None]

    conv_size = conv_part.size
    small = jnp.concatenate([conv_part.reshape(-1), gain_part]).reshape(-1, row_width)
    small = butterfly_sum(small, "seq")
    panel_part, small, grad_bytes = lax.optimization_barrier((panel_part, small, grad_bytes))
    fsdp_count = lax.axis_size("fsdp")
    partner_pairs = [(i, i ^ 1) for i in range(fsdp_count)]
    padded_rows = 2 * (-(-small.shape[0] // 16) * 8)
    small = jnp.pad(small, ((0, padded_rows - small.shape[0]), (0, 0)))
    upper_core = lax.axis_index("fsdp") % 2 == 1
    kept = jnp.where(upper_core, small[padded_rows // 2 :], small[: padded_rows // 2])
    given = jnp.where(upper_core, small[: padded_rows // 2], small[padded_rows // 2 :])
    fsdp_levels = fsdp_count.bit_length() - 1
    seq_levels = lax.axis_size("seq").bit_length() - 1
    for level in range(seq_levels):
        panel_part = butterfly_sum(panel_part, "seq", level, level + 1)
        if level == 0:
            kept = kept + lax.ppermute(given, "fsdp", partner_pairs)
            kept = butterfly_sum(kept, "fsdp", 1, 2)
        elif level < fsdp_levels - 1:
            kept = butterfly_sum(kept, "fsdp", level + 1, level + 2)
        else:
            other = lax.ppermute(kept, "fsdp", partner_pairs)
            small = jnp.where(
                upper_core,
                jnp.concatenate([other, kept], 0),
                jnp.concatenate([kept, other], 0),
            )
        panel_part, kept = lax.optimization_barrier((panel_part, kept))
    proj_sum = panel_part
    small_sum = small.reshape(-1)
    conv_sum = small_sum[:conv_size].reshape(conv_part.shape)
    gain_sum = small_sum[conv_size : conv_size + row_width]

    total_patches = patches * lax.axis_size("seq") * lax.axis_size("fsdp")
    grad_scale = 1.0 / math.sqrt(total_patches)
    first_panel = lax.axis_index("fsdp") * jnp.int32(panel_rows)
    row_index = first_panel + jnp.arange(panel_rows, dtype=jnp.int32)
    flat_index = (
        row_index[:, None] * jnp.int32(row_width) + jnp.arange(row_width, dtype=jnp.int32)[None, :]
    )
    dither_noise = mix_bits(flat_index, round_seed[0], step_count[0])
    grad_proj = proj_sum * grad_scale + QUANT * (dither_noise - 0.5)
    return (grad_bytes, grad_proj, conv_sum * grad_scale, gain_sum * grad_scale)


def solution(mesh):
    in_specs = (
        P("fsdp", "seq", None),
        P("fsdp", "seq", None),
        P("fsdp", "seq"),
        P(),
        P(),
        P("fsdp", None),
        P(),
        P(),
    )
    out_specs = (P("fsdp", "seq", None), P("fsdp", None), P(), P())
    return jax.shard_map(
        per_device, mesh=mesh, in_specs=in_specs, out_specs=out_specs, check_vma=False
    )
```

```python
import math

import jax
import jax.numpy as jnp
from jax import lax
from jax.sharding import PartitionSpec as P

GROUPS = 32
KERNEL = 8
STRIDE = 4
CG = 16


GELU_A = 0.7978845608028654
GELU_B = 0.044715
QUANT = 0.25


def shifted(value, axis, steps):
    count = lax.axis_size(axis)
    initial, last = (max(0, -steps), min(count, count - steps))
    return lax.ppermute(value, axis, [(source, source + steps) for source in range(initial, last)])


def gelu_grad(values):
    tangent = jnp.tanh(GELU_A * (values + GELU_B * values * values * values))
    return 0.5 * (1.0 + tangent) + 0.5 * values * (1.0 - tangent * tangent) * GELU_A * (
        1.0 + 3.0 * GELU_B * values * values
    )


def mix_bits(flat_index, seed_value, step_value):
    hashed = (
        flat_index * jnp.int32(-1640531535)
        + seed_value * jnp.int32(-2048144777)
        + step_value * jnp.int32(-1028477379)
    )
    hashed = hashed ^ lax.shift_right_logical(hashed, jnp.int32(16))
    hashed = hashed * jnp.int32(2146121005)
    hashed = hashed ^ lax.shift_right_logical(hashed, jnp.int32(15))
    hashed = hashed * jnp.int32(-2073254261)
    hashed = hashed ^ lax.shift_right_logical(hashed, jnp.int32(16))
    return lax.shift_right_logical(hashed, jnp.int32(8)).astype(jnp.float32) / 16777216.0


def butterfly_sum(value, axis, first=0, last=None):
    count = lax.axis_size(axis)
    last = count.bit_length() - 1 if last is None else last
    for level in range(first, last):
        distance = 1 << level
        partner = lax.ppermute(value, axis, [(i, i ^ distance) for i in range(count)])
        value = value + partner
    return value


def split_bf16(value):
    high = lax.reduce_precision(value, exponent_bits=8, mantissa_bits=7)
    low = (value - high).astype(jnp.bfloat16)
    return high.astype(jnp.bfloat16), low


def dot_f32(lhs, rhs, dims):
    return lax.dot_general(lhs, rhs, (dims, ((), ())), preferred_element_type=jnp.float32)


def per_device(
    byte_rows, cotangent, doc_ids, conv_weight, norm_gain, proj_weight, round_seed, step_count
):
    byte_block = byte_rows[0]
    upstream = cotangent[0]
    doc_block = doc_ids[0]
    length = byte_block.shape[0]
    row_width = byte_block.shape[1]
    patches = length // STRIDE
    half = STRIDE * row_width
    panel_rows = proj_weight.shape[0]
    next_bytes, next_up, next_docs = shifted(
        (byte_block[:STRIDE], upstream[:STRIDE], doc_block[:STRIDE]), "seq", -1
    )
    bytes_lo = byte_block.reshape(patches, half)
    bytes_hi = jnp.concatenate([bytes_lo[1:], next_bytes.reshape(1, half)], 0)
    up_lo = upstream.reshape(patches, half)
    up_hi = jnp.concatenate([up_lo[1:], next_up.reshape(1, half)], 0)
    docs_lo = doc_block.reshape(patches, STRIDE)
    docs_hi = jnp.concatenate([docs_lo[1:], next_docs.reshape(1, STRIDE)], 0)
    is_last = lax.axis_index("seq") == lax.axis_size("seq") - 1
    patch_ids = lax.broadcasted_iota(jnp.int32, (patches, STRIDE), 0)
    spilled = is_last & (patch_ids == patches - 1)
    keep_lo = docs_lo == docs_lo[:, :1]
    keep_hi = (docs_hi == docs_lo[:, :1]) & jnp.logical_not(spilled)

    def spread(keep):
        return jnp.broadcast_to(keep[:, :, None], (patches, STRIDE, row_width)).reshape(
            patches, half
        )

    keep_lo_f = spread(keep_lo.astype(jnp.float32))
    keep_hi_f = spread(keep_hi.astype(jnp.float32))
    win_lo = bytes_lo * keep_lo_f.astype(jnp.bfloat16)
    win_hi = bytes_hi * keep_hi_f.astype(jnp.bfloat16)

    tile_rows = lax.broadcasted_iota(jnp.int32, (CG, row_width), 0)
    tile_cols = lax.broadcasted_iota(jnp.int32, (CG, row_width), 1)
    tiler = (tile_cols % CG == tile_rows).astype(jnp.bfloat16)
    tiled = dot_f32(conv_weight.reshape(KERNEL * row_width, CG), tiler, ((1,), (0,)))
    block_rows = lax.broadcasted_iota(jnp.int32, (half, row_width), 0)
    block_cols = lax.broadcasted_iota(jnp.int32, (half, row_width), 1)
    on_block = (block_rows % row_width) // CG == block_cols // CG
    dense_weight = tiled.reshape(2, half, row_width)
    weight_lo = jnp.where(on_block, dense_weight[0], 0.0).astype(jnp.bfloat16)
    weight_hi = jnp.where(on_block, dense_weight[1], 0.0).astype(jnp.bfloat16)

    hidden = dot_f32(win_lo, weight_lo, ((1,), (0,))) + dot_f32(win_hi, weight_hi, ((1,), (0,)))
    factor = lax.rsqrt(jnp.mean(hidden * hidden, axis=-1, keepdims=True) + 1e-06)
    normed = (hidden * factor * norm_gain).astype(jnp.bfloat16)

    full_proj = lax.all_gather(proj_weight, "fsdp", axis=0, tiled=True)
    proj_lo = full_proj[:half]
    proj_hi = full_proj[half:]
    pre_lo = dot_f32(normed, proj_lo, ((1,), (1,)))
    pre_hi = dot_f32(normed, proj_hi, ((1,), (1,)))
    grad_pre_lo = (up_lo.astype(jnp.float32) * keep_lo_f * gelu_grad(pre_lo)).astype(jnp.bfloat16)
    grad_pre_hi = (up_hi.astype(jnp.float32) * keep_hi_f * gelu_grad(pre_hi)).astype(jnp.bfloat16)

    grad_pre = jnp.concatenate([grad_pre_lo, grad_pre_hi], 1)
    proj_part = dot_f32(grad_pre, normed, ((0,), (0,)))
    panel_part = lax.psum_scatter(proj_part, "fsdp", scatter_dimension=0, tiled=True)

    grad_norm = dot_f32(grad_pre_lo, proj_lo, ((1,), (0,))) + dot_f32(
        grad_pre_hi, proj_hi, ((1,), (0,))
    )
    gain_part = jnp.sum(grad_norm * hidden * factor, axis=0)
    gained = norm_gain * grad_norm
    grad_hidden = factor * gained - hidden * factor * factor * factor * jnp.mean(
        gained * hidden, axis=-1, keepdims=True
    )
    gh_high, gh_low = split_bf16(grad_hidden)

    def window_grad(window):
        full = dot_f32(window, gh_high, ((0,), (0,))) + dot_f32(window, gh_low, ((0,), (0,)))
        diagonal = lax.dot_general(
            jnp.where(on_block, full, 0.0),
            tiler.astype(jnp.float32),
            (((1,), (1,)), ((), ())),
            precision=lax.Precision.HIGHEST,
            preferred_element_type=jnp.float32,
        )
        return diagonal.reshape(STRIDE, GROUPS, CG, CG)

    conv_part = jnp.concatenate([window_grad(win_lo), window_grad(win_hi)], 0)

    def back_taps(weight, keep_f):
        taps = dot_f32(gh_high, weight, ((1,), (1,))) + dot_f32(gh_low, weight, ((1,), (1,)))
        return (taps * keep_f).reshape(length, row_width)

    back_lower = back_taps(weight_lo, keep_lo_f)
    back_upper = back_taps(weight_hi, keep_hi_f)
    incoming = shifted(back_upper[length - STRIDE :], "seq", 1)
    back_rows = back_lower + jnp.concatenate([incoming, back_upper[: length - STRIDE]], 0)
    grad_bytes = (upstream.astype(jnp.float32) + back_rows)[None]

    conv_size = conv_part.size
    small = jnp.concatenate([conv_part.reshape(-1), gain_part]).reshape(-1, row_width)
    small = butterfly_sum(small, "seq")
    panel_part, small, grad_bytes = lax.optimization_barrier((panel_part, small, grad_bytes))
    fsdp_count = lax.axis_size("fsdp")
    partner_pairs = [(i, i ^ 1) for i in range(fsdp_count)]
    padded_rows = 2 * (-(-small.shape[0] // 16) * 8)
    small = jnp.pad(small, ((0, padded_rows - small.shape[0]), (0, 0)))
    upper_core = lax.axis_index("fsdp") % 2 == 1
    kept = jnp.where(upper_core, small[padded_rows // 2 :], small[: padded_rows // 2])
    given = jnp.where(upper_core, small[: padded_rows // 2], small[padded_rows // 2 :])
    fsdp_levels = fsdp_count.bit_length() - 1
    seq_count = lax.axis_size("seq")
    seq_levels = seq_count.bit_length() - 1
    seq_pairs = [(i, i ^ 1) for i in range(seq_count)]
    upper_seq = lax.axis_index("seq") % 2 == 1
    split_rows = panel_part.shape[0] // 2
    kept_rows = jnp.where(upper_seq, panel_part[split_rows:], panel_part[:split_rows])
    given_rows = jnp.where(upper_seq, panel_part[:split_rows], panel_part[split_rows:])
    for group in range(seq_levels + 1):
        if group == 0:
            kept_rows = kept_rows + lax.ppermute(given_rows, "seq", seq_pairs)
        elif group < seq_levels:
            kept_rows = butterfly_sum(kept_rows, "seq", group, group + 1)
        else:
            other_rows = lax.ppermute(kept_rows, "seq", seq_pairs)
            panel_part = jnp.where(
                upper_seq,
                jnp.concatenate([other_rows, kept_rows], 0),
                jnp.concatenate([kept_rows, other_rows], 0),
            )
        if group == 0:
            kept = kept + lax.ppermute(given, "fsdp", partner_pairs)
            kept = butterfly_sum(kept, "fsdp", 1, 2)
        elif group < fsdp_levels - 1:
            kept = butterfly_sum(kept, "fsdp", group + 1, group + 2)
        elif group == fsdp_levels - 1:
            other = lax.ppermute(kept, "fsdp", partner_pairs)
            small = jnp.where(
                upper_core,
                jnp.concatenate([other, kept], 0),
                jnp.concatenate([kept, other], 0),
            )
        kept_rows, kept = lax.optimization_barrier((kept_rows, kept))
    proj_sum = panel_part
    small_sum = small.reshape(-1)
    conv_sum = small_sum[:conv_size].reshape(conv_part.shape)
    gain_sum = small_sum[conv_size : conv_size + row_width]

    total_patches = patches * lax.axis_size("seq") * lax.axis_size("fsdp")
    grad_scale = 1.0 / math.sqrt(total_patches)
    first_panel = lax.axis_index("fsdp") * jnp.int32(panel_rows)
    row_index = first_panel + jnp.arange(panel_rows, dtype=jnp.int32)
    flat_index = (
        row_index[:, None] * jnp.int32(row_width) + jnp.arange(row_width, dtype=jnp.int32)[None, :]
    )
    dither_noise = mix_bits(flat_index, round_seed[0], step_count[0])
    grad_proj = proj_sum * grad_scale + QUANT * (dither_noise - 0.5)
    return (grad_bytes, grad_proj, conv_sum * grad_scale, gain_sum * grad_scale)


def solution(mesh):
    in_specs = (
        P("fsdp", "seq", None),
        P("fsdp", "seq", None),
        P("fsdp", "seq"),
        P(),
        P(),
        P("fsdp", None),
        P(),
        P(),
    )
    out_specs = (P("fsdp", "seq", None), P("fsdp", None), P(), P())
    return jax.shard_map(
        per_device, mesh=mesh, in_specs=in_specs, out_specs=out_specs, check_vma=False
    )
```

```python
import math

import jax
import jax.numpy as jnp
from jax import lax
from jax.sharding import PartitionSpec as P

GROUPS = 32
KERNEL = 8
STRIDE = 4
CG = 16


GELU_A = 0.7978845608028654
GELU_B = 0.044715
QUANT = 0.25


def shifted(value, axis, steps):
    count = lax.axis_size(axis)
    initial, last = (max(0, -steps), min(count, count - steps))
    return lax.ppermute(value, axis, [(source, source + steps) for source in range(initial, last)])


def gelu_grad(values):
    tangent = jnp.tanh(GELU_A * (values + GELU_B * values * values * values))
    return 0.5 * (1.0 + tangent) + 0.5 * values * (1.0 - tangent * tangent) * GELU_A * (
        1.0 + 3.0 * GELU_B * values * values
    )


def mix_bits(flat_index, seed_value, step_value):
    hashed = (
        flat_index * jnp.int32(-1640531535)
        + seed_value * jnp.int32(-2048144777)
        + step_value * jnp.int32(-1028477379)
    )
    hashed = hashed ^ lax.shift_right_logical(hashed, jnp.int32(16))
    hashed = hashed * jnp.int32(2146121005)
    hashed = hashed ^ lax.shift_right_logical(hashed, jnp.int32(15))
    hashed = hashed * jnp.int32(-2073254261)
    hashed = hashed ^ lax.shift_right_logical(hashed, jnp.int32(16))
    return lax.shift_right_logical(hashed, jnp.int32(8)).astype(jnp.float32) / 16777216.0


def butterfly_sum(value, axis, first=0, last=None):
    count = lax.axis_size(axis)
    last = count.bit_length() - 1 if last is None else last
    for level in range(first, last):
        distance = 1 << level
        partner = lax.ppermute(value, axis, [(i, i ^ distance) for i in range(count)])
        value = value + partner
    return value


def split_bf16(value):
    high = lax.reduce_precision(value, exponent_bits=8, mantissa_bits=7)
    low = (value - high).astype(jnp.bfloat16)
    return high.astype(jnp.bfloat16), low


def dot_f32(lhs, rhs, dims):
    return lax.dot_general(lhs, rhs, (dims, ((), ())), preferred_element_type=jnp.float32)


def per_device(
    byte_rows, cotangent, doc_ids, conv_weight, norm_gain, proj_weight, round_seed, step_count
):
    byte_block = byte_rows[0]
    upstream = cotangent[0]
    doc_block = doc_ids[0]
    length = byte_block.shape[0]
    row_width = byte_block.shape[1]
    patches = length // STRIDE
    half = STRIDE * row_width
    panel_rows = proj_weight.shape[0]
    next_bytes, next_up, next_docs = shifted(
        (byte_block[:STRIDE], upstream[:STRIDE], doc_block[:STRIDE]), "seq", -1
    )
    bytes_lo = byte_block.reshape(patches, half)
    bytes_hi = jnp.concatenate([bytes_lo[1:], next_bytes.reshape(1, half)], 0)
    up_lo = upstream.reshape(patches, half)
    up_hi = jnp.concatenate([up_lo[1:], next_up.reshape(1, half)], 0)
    docs_lo = doc_block.reshape(patches, STRIDE)
    docs_hi = jnp.concatenate([docs_lo[1:], next_docs.reshape(1, STRIDE)], 0)
    is_last = lax.axis_index("seq") == lax.axis_size("seq") - 1
    patch_ids = lax.broadcasted_iota(jnp.int32, (patches, STRIDE), 0)
    spilled = is_last & (patch_ids == patches - 1)
    keep_lo = docs_lo == docs_lo[:, :1]
    keep_hi = (docs_hi == docs_lo[:, :1]) & jnp.logical_not(spilled)

    def spread(keep):
        return jnp.broadcast_to(keep[:, :, None], (patches, STRIDE, row_width)).reshape(
            patches, half
        )

    keep_lo_f = spread(keep_lo.astype(jnp.float32))
    keep_hi_f = spread(keep_hi.astype(jnp.float32))
    win_lo = bytes_lo * keep_lo_f.astype(jnp.bfloat16)
    win_hi = bytes_hi * keep_hi_f.astype(jnp.bfloat16)

    tile_rows = lax.broadcasted_iota(jnp.int32, (CG, row_width), 0)
    tile_cols = lax.broadcasted_iota(jnp.int32, (CG, row_width), 1)
    tiler = (tile_cols % CG == tile_rows).astype(jnp.bfloat16)
    tiled = dot_f32(conv_weight.reshape(KERNEL * row_width, CG), tiler, ((1,), (0,)))
    block_rows = lax.broadcasted_iota(jnp.int32, (half, row_width), 0)
    block_cols = lax.broadcasted_iota(jnp.int32, (half, row_width), 1)
    on_block = (block_rows % row_width) // CG == block_cols // CG
    dense_weight = tiled.reshape(2, half, row_width)
    weight_lo = jnp.where(on_block, dense_weight[0], 0.0).astype(jnp.bfloat16)
    weight_hi = jnp.where(on_block, dense_weight[1], 0.0).astype(jnp.bfloat16)

    hidden = dot_f32(win_lo, weight_lo, ((1,), (0,))) + dot_f32(win_hi, weight_hi, ((1,), (0,)))
    factor = lax.rsqrt(jnp.mean(hidden * hidden, axis=-1, keepdims=True) + 1e-06)
    normed = (hidden * factor * norm_gain).astype(jnp.bfloat16)

    full_proj = lax.all_gather(proj_weight, "fsdp", axis=0, tiled=True)
    proj_lo = full_proj[:half]
    proj_hi = full_proj[half:]
    pre_lo = dot_f32(normed, proj_lo, ((1,), (1,)))
    pre_hi = dot_f32(normed, proj_hi, ((1,), (1,)))
    grad_pre_lo = (up_lo.astype(jnp.float32) * keep_lo_f * gelu_grad(pre_lo)).astype(jnp.bfloat16)
    grad_pre_hi = (up_hi.astype(jnp.float32) * keep_hi_f * gelu_grad(pre_hi)).astype(jnp.bfloat16)

    grad_pre = jnp.concatenate([grad_pre_lo, grad_pre_hi], 1)
    proj_part = dot_f32(grad_pre, normed, ((0,), (0,)))
    panel_part = lax.psum_scatter(proj_part, "fsdp", scatter_dimension=0, tiled=True)

    grad_norm = dot_f32(grad_pre_lo, proj_lo, ((1,), (0,))) + dot_f32(
        grad_pre_hi, proj_hi, ((1,), (0,))
    )
    gain_part = jnp.sum(grad_norm * hidden * factor, axis=0)
    gained = norm_gain * grad_norm
    grad_hidden = factor * gained - hidden * factor * factor * factor * jnp.mean(
        gained * hidden, axis=-1, keepdims=True
    )
    gh_high, gh_low = split_bf16(grad_hidden)

    def window_grad(window):
        full = dot_f32(window, gh_high, ((0,), (0,))) + dot_f32(window, gh_low, ((0,), (0,)))
        diagonal = lax.dot_general(
            jnp.where(on_block, full, 0.0),
            tiler.astype(jnp.float32),
            (((1,), (1,)), ((), ())),
            precision=lax.Precision.HIGHEST,
            preferred_element_type=jnp.float32,
        )
        return diagonal.reshape(STRIDE, GROUPS, CG, CG)

    conv_part = jnp.concatenate([window_grad(win_lo), window_grad(win_hi)], 0)

    def back_taps(weight, keep_f):
        taps = dot_f32(gh_high, weight, ((1,), (1,))) + dot_f32(gh_low, weight, ((1,), (1,)))
        return (taps * keep_f).reshape(length, row_width)

    back_lower = back_taps(weight_lo, keep_lo_f)
    back_upper = back_taps(weight_hi, keep_hi_f)
    incoming = shifted(back_upper[length - STRIDE :], "seq", 1)
    back_rows = back_lower + jnp.concatenate([incoming, back_upper[: length - STRIDE]], 0)
    grad_bytes = (upstream.astype(jnp.float32) + back_rows)[None]

    conv_size = conv_part.size
    small = jnp.concatenate([conv_part.reshape(-1), gain_part]).reshape(-1, row_width)
    small = butterfly_sum(small, "seq")
    panel_part, small, grad_bytes = lax.optimization_barrier((panel_part, small, grad_bytes))
    quarter = -(-small.shape[0] // 32) * 8
    small = jnp.pad(small, ((0, 4 * quarter - small.shape[0]), (0, 0)))
    fsdp_levels = lax.axis_size("fsdp").bit_length() - 1
    seq_levels = lax.axis_size("seq").bit_length() - 1

    def pairs(axis, bit):
        return [(i, i ^ (1 << bit)) for i in range(lax.axis_size(axis))]

    def halve(value, axis, bit):
        upper = (lax.axis_index(axis) >> bit) % 2 == 1
        rows = value.shape[0] // 2
        kept = jnp.where(upper, value[rows:], value[:rows])
        given = jnp.where(upper, value[:rows], value[rows:])
        return kept + lax.ppermute(given, axis, pairs(axis, bit))

    def regather(value, axis, bit):
        upper = (lax.axis_index(axis) >> bit) % 2 == 1
        other = lax.ppermute(value, axis, pairs(axis, bit))
        return jnp.where(
            upper, jnp.concatenate([other, value], 0), jnp.concatenate([value, other], 0)
        )

    conv_stages = [lambda v: halve(halve(v, "fsdp", 0), "fsdp", 1)]
    conv_stages += [
        lambda v, level=level: butterfly_sum(v, "fsdp", level, level + 1)
        for level in range(2, fsdp_levels)
    ]
    conv_stages += [lambda v: regather(v, "fsdp", 1), lambda v: regather(v, "fsdp", 0)]
    proj_stages = [lambda v: halve(v, "seq", 0)]
    proj_stages += [
        lambda v, level=level: butterfly_sum(v, "seq", level, level + 1)
        for level in range(1, seq_levels)
    ]
    proj_stages += [lambda v: regather(v, "seq", 0)]
    stage_count = max(len(conv_stages), len(proj_stages))
    for stage in range(stage_count):
        if stage < len(proj_stages):
            panel_part = proj_stages[stage](panel_part)
        if stage < len(conv_stages):
            small = conv_stages[stage](small)
        panel_part, small = lax.optimization_barrier((panel_part, small))
    proj_sum = panel_part
    small_sum = small.reshape(-1)
    conv_sum = small_sum[:conv_size].reshape(conv_part.shape)
    gain_sum = small_sum[conv_size : conv_size + row_width]

    total_patches = patches * lax.axis_size("seq") * lax.axis_size("fsdp")
    grad_scale = 1.0 / math.sqrt(total_patches)
    first_panel = lax.axis_index("fsdp") * jnp.int32(panel_rows)
    row_index = first_panel + jnp.arange(panel_rows, dtype=jnp.int32)
    flat_index = (
        row_index[:, None] * jnp.int32(row_width) + jnp.arange(row_width, dtype=jnp.int32)[None, :]
    )
    dither_noise = mix_bits(flat_index, round_seed[0], step_count[0])
    grad_proj = proj_sum * grad_scale + QUANT * (dither_noise - 0.5)
    return (grad_bytes, grad_proj, conv_sum * grad_scale, gain_sum * grad_scale)


def solution(mesh):
    in_specs = (
        P("fsdp", "seq", None),
        P("fsdp", "seq", None),
        P("fsdp", "seq"),
        P(),
        P(),
        P("fsdp", None),
        P(),
        P(),
    )
    out_specs = (P("fsdp", "seq", None), P("fsdp", None), P(), P())
    return jax.shard_map(
        per_device, mesh=mesh, in_specs=in_specs, out_specs=out_specs, check_vma=False
    )
```
